256 devices in a mesh: group: 8 (over y, core), expert: 32 (over z, x).
Axes of the slice: x: 4, y: 4, z: 8, core: 2. Of those that a mesh axis runs over, the one named last changes fastest.
Arguments:
- context: bfloat16 [32768, 1024], P(('group', 'expert')), may hold values from -6 to 6
- residual: bfloat16 [32768, 2048], P(('group', 'expert')), may hold values from -0.8984375 to 0.8984375
- attn_out_w: bfloat16 [1024, 2048], P('group'), may hold values from -0.02734375 to 0.02734375
- norm_gain: float32 [2048], replicated, may hold values from 0.25 to 1.75
- router_w: bfloat16 [2048, 32], replicated, may hold values from -0.047851562 to 0.047851562
- shared_in: bfloat16 [2048, 2816], P('group'), may hold values from -0.125 to 0.125
- shared_out: bfloat16 [1408, 2048], P(None, 'group'), may hold values from -0.0234375 to 0.0234375
- expert_in: bfloat16 [32, 2048, 1536], P('expert'), may hold values from -0.125 to 0.125
- expert_out_w: bfloat16 [32, 768, 2048], P('expert'), may hold values from -0.21875 to 0.21875
- routes: int32 [32768, 6], P(('group', 'expert')), may hold values from 0 to 31, all different within a row; in each aligned block of 128 rows (0 to 127, 128 to 255, ...) at most 32 rows name the same one
Outputs:
- layer_out: bfloat16 [32768, 2048], P(('group', 'expert'))
The draws below stay inside these ranges and needn't reach their ends.
Inputs may be any that keep to these rules, and one draw needn't show every extreme that they name: `routes`: the 6 experts of a token differ. Among the rows of one device, no expert is named by more than 32 rows, a bound that some block reaches.
All inputs are finite; a program needn't handle non-finite values.
Results may differ from the reference program's by a relative error of at most 0.022.
Values may be sent and summed in bfloat16 or wider, within the bound.
No kernel may reach another device: no remote copies, remote signals or barrier semaphores. Data moves between devices by JAX's collectives and lax.ppermute only.
A program may use at most 128 MiB of HBM per device.

```python
import math
import jax
import jax.numpy as jnp
import numpy as np
from jax import lax

D = 2048
HEADS = 8
HDIM = 128
FFW = 768
SFF = 1408
TOP = 6
TOK_DEV = 128
EXPERTS = 32
CAP = 32
TOKENS = 32768
N_GROUP = 8
N_EXPERT = 32


def block_levels(stream_key, shape, pieces, least, top_value):
    def one(dim, shards_of):
        draws = jax.random.uniform(jax.random.fold_in(jax.random.fold_in(stream_key, 6), dim), (shards_of,), jnp.float32, least / len(pieces), top_value / len(pieces))
        return jnp.repeat(jnp.exp(draws), shape[dim] // shards_of).reshape((-1,) + (1,) * (len(shape) - dim - 1))

    gain = one(*pieces[0])
    for cut in pieces[1:]:
        gain = gain * one(*cut)
    return gain


def routed_block(own_key, own, number, rows, amount, top, reach, skew):
    order = jax.random.permutation(own_key, amount)
    crowded, usual = shares(amount, rows * top, reach, skew, True), shares(amount, rows * top, reach, skew, False)
    places = jnp.arange(amount)

    def named(lengths, turn):
        used = int((lengths > 0).sum())
        fixed = max(1, used // 4)
        shifted = fixed + (places - fixed + turn * (used - fixed)) % max(1, amount - fixed)
        return jnp.zeros((amount,), jnp.int32).at[order[jnp.where(places < fixed, places, shifted)]].set(jnp.asarray(lengths, jnp.int32))

    lengths = jnp.where(number % 4 == 0, named(crowded, number // 4), named(usual, number - number // 4 - 1))
    mixed = jax.random.permutation(jax.random.fold_in(own, 3), amount)
    giver, receiver = mixed[0:amount // 2 * 2:2], mixed[1:amount // 2 * 2:2]
    room = jnp.minimum(lengths[giver] - 1, reach - lengths[receiver]) // 2
    room = jnp.where((giver == order[0]) | (receiver == order[0]) | (lengths[receiver] == 0), 0, jnp.maximum(room, 0))
    shifted = jax.random.randint(jax.random.fold_in(own, 4), (amount // 2,), 0, 1 << 20) % (room + 1)
    lengths = lengths.at[giver].add(-shifted).at[receiver].add(shifted)
    members = jnp.searchsorted(jnp.cumsum(lengths), jnp.arange(rows * top), side="right").astype(jnp.int32)
    grid = members.reshape(top, rows).T
    grid = grid[jax.random.permutation(jax.random.fold_in(own, 1), rows)]
    turn = jax.random.randint(jax.random.fold_in(own, 2), (rows, 1), 0, top)
    return jnp.take_along_axis(grid, (jnp.arange(top)[None, :] + turn) % top, axis=1)


def shares(amount, total, reach, slope, full):
    loads = [(1 << 20) // math.isqrt(standing ** slope) + 1 for standing in range(1, amount + 1)]
    largest = reach if full else min(reach, max(-(-total // amount), total * loads[0] // sum(loads)))
    least = 1 if total - largest >= amount - 1 else 0
    given, surplus = [largest] + [least] * (amount - 1), total - largest - least * (amount - 1)
    while surplus > 0:
        free = [i for i in range(1, amount) if given[i] < largest] or [i for i in range(1, amount) if given[i] < reach]
        pool, left = sum([loads[i] for i in free]), surplus
        for i in free:
            addition = min(reach - given[i], max(1, left * loads[i] // pool), surplus)
            given[i] = given[i] + addition
            surplus = surplus - addition
    return np.array(given)


def noise(key, extent, scale, reach, shards=(), kind=jnp.bfloat16):
    loudness = block_levels(key, extent, shards, -0.22, 0.18) if shards else 1.0
    values = jax.random.normal(key, extent, jnp.float32) * scale * loudness
    return jnp.minimum(jnp.maximum(values, -reach), reach).astype(kind)


def setup_inputs(seed: int = 0) -> dict:
    streams_of = jax.random.split(jax.random.key(seed), 11)
    context = noise(streams_of[0], (TOKENS, HEADS * HDIM), 1.0, 6.0, ((0, 256),))
    residual = noise(streams_of[1], (TOKENS, D), 0.15, 0.8984375, ((0, 256),))
    attn_out_w = noise(streams_of[2], (HEADS * HDIM, D), (44 * HEADS * HDIM) ** -0.5, 0.02734375, ((0, 8),))
    norm_gain = jnp.clip(1.0 + 0.15 * jax.random.normal(streams_of[3], (D,), jnp.float32), 0.25, 1.75)
    router_w = noise(streams_of[4], (D, EXPERTS), 0.012, 0.047851562)
    shared_in = noise(streams_of[5], (D, 2 * SFF), D ** -0.5, 0.125, ((0, 8),))
    shared_out = noise(streams_of[6], (SFF, D), (44 * SFF) ** -0.5, 0.0234375, ((1, 8),))
    expert_in = noise(streams_of[7], (EXPERTS, D, 2 * FFW), D ** -0.5, 0.125, ((0, 32),))
    expert_out_w = noise(streams_of[8], (EXPERTS, FFW, D), FFW ** -0.5, 0.21875, ((0, 32),))
    routes_keys = jax.random.split(jax.random.fold_in(streams_of[9], 1), TOKENS // TOK_DEV)
    routes_turns = jax.random.permutation(jax.random.fold_in(streams_of[9], 3), TOKENS // TOK_DEV)
    routes = jax.vmap(lambda own, number: routed_block(jax.random.fold_in(streams_of[9], 2), own, number, TOK_DEV, EXPERTS, TOP, CAP, 2))(routes_keys, routes_turns).reshape((TOKENS, TOP))
    return {"context": context, "residual": residual, "attn_out_w": attn_out_w, "norm_gain": norm_gain, "router_w": router_w, "shared_in": shared_in, "shared_out": shared_out, "expert_in": expert_in, "expert_out_w": expert_out_w, "routes": routes}


def swiglu_rows(rows, w_in, w_out):
    width = w_out.shape[0]
    mid = jnp.dot(rows, w_in, preferred_element_type=jnp.float32)
    act = (jax.nn.silu(mid[:, :width]) * mid[:, width:]).astype(jnp.bfloat16)
    return jnp.dot(act, w_out, preferred_element_type=jnp.float32)

def reference(context, residual, attn_out_w, norm_gain, router_w, shared_in, shared_out, expert_in, expert_out_w, routes):
    attn = jnp.dot(context, attn_out_w, preferred_element_type=jnp.float32)
    hidden_state = (residual.astype(jnp.float32) + attn).astype(jnp.bfloat16)
    hidden_f = hidden_state.astype(jnp.float32)
    scale = lax.rsqrt(lax.optimization_barrier(jnp.mean(hidden_f * hidden_f, axis=-1, keepdims=True)) + 1e-06)
    normed = (hidden_f * scale * norm_gain).astype(jnp.bfloat16)
    logits = jnp.dot(normed, router_w, preferred_element_type=jnp.float32)
    picked = jnp.take_along_axis(logits, routes, axis=1)
    sig = jax.nn.sigmoid(picked)
    gates = sig / lax.optimization_barrier(jnp.sum(sig, axis=1, keepdims=True))
    shared_y = swiglu_rows(normed, shared_in, shared_out)
    devices = N_GROUP * N_EXPERT
    per = TOK_DEV * TOP
    total = TOKENS * TOP
    flat_e = routes.reshape(-1).astype(jnp.int32)
    onehot = (flat_e[:, None] == jnp.arange(EXPERTS, dtype=jnp.int32)[None, :]).astype(jnp.int32)
    blocked = onehot.reshape(devices, per, EXPERTS)
    rank = jnp.cumsum(blocked, axis=1) - blocked
    position = lax.optimization_barrier(jnp.sum(rank * blocked, axis=-1)).reshape(-1).astype(jnp.int32)
    flat_idx = jnp.arange(total, dtype=jnp.int32)
    device = flat_idx // per
    token = flat_idx // TOP
    gate_flat = gates.reshape(-1)

    def one_expert(acc, expert):
        target = jnp.where(flat_e == expert, device * CAP + position, devices * CAP).astype(jnp.int32)
        source = jnp.zeros((devices * CAP,), jnp.int32).at[target].set(token, mode='drop')
        weight = jnp.zeros((devices * CAP,), jnp.float32).at[target].set(gate_flat, mode='drop')
        rows = normed[source]
        out = swiglu_rows(rows, expert_in[expert], expert_out_w[expert]).astype(jnp.bfloat16)
        acc = acc.at[source].add(weight[:, None] * out.astype(jnp.float32))
        return (acc, None)
    routed, _ = lax.scan(one_expert, jnp.zeros((TOKENS, D), jnp.float32), jnp.arange(EXPERTS, dtype=jnp.int32))
    return (hidden_f + shared_y + routed).astype(jnp.bfloat16)
```

```python
import jax
import jax.numpy as jnp
from jax import lax
from jax.sharding import PartitionSpec as P


def swiglu_rows(rows, w_in, w_out):
    width = w_out.shape[0]
    mid = jnp.dot(rows, w_in, preferred_element_type=jnp.float32)
    act = (jax.nn.silu(mid[:, :width]) * mid[:, width:]).astype(jnp.bfloat16)
    return jnp.dot(act, w_out, preferred_element_type=jnp.float32)


def per_device(
    context,
    residual,
    attn_out_w,
    norm_gain,
    router_w,
    shared_in,
    shared_out,
    expert_in,
    expert_out_w,
    routes,
):
    tok_rows = residual.shape[0]
    width = residual.shape[1]
    picks = routes.shape[1]
    experts = lax.axis_size("expert")
    capacity = 4 * tok_rows * picks // (3 * experts)
    slots = experts * capacity
    attn = jnp.dot(
        context,
        lax.all_gather(attn_out_w, "group", axis=0, tiled=True),
        preferred_element_type=jnp.float32,
    )
    hidden_state = (residual.astype(jnp.float32) + attn).astype(jnp.bfloat16)
    hidden_f = hidden_state.astype(jnp.float32)
    scale = lax.rsqrt(jnp.mean(hidden_f * hidden_f, axis=-1, keepdims=True) + 1e-06)
    normed = (hidden_f * scale * norm_gain).astype(jnp.bfloat16)
    logits = jnp.dot(normed, router_w, preferred_element_type=jnp.float32)
    chosen = routes[:, :, None] == jnp.arange(experts, dtype=jnp.int32)[None, None, :]
    picked = jnp.sum(jnp.where(chosen, logits[:, None, :], 0.0), axis=-1)
    sig = jax.nn.sigmoid(picked)
    gates = sig / jnp.sum(sig, axis=1, keepdims=True)
    flat_e = routes.reshape(-1)
    onehot = (flat_e[:, None] == jnp.arange(experts, dtype=jnp.int32)[None, :]).astype(jnp.int32)
    rank = jnp.cumsum(onehot, axis=0) - onehot
    position = jnp.sum(rank * onehot, axis=1)
    slot_of = (flat_e * capacity + position).reshape(tok_rows, picks)
    hit = slot_of[:, :, None] == jnp.arange(slots, dtype=jnp.int32)[None, None, :]
    dispatch = jnp.any(hit, axis=1).astype(jnp.bfloat16)
    outgoing = jnp.dot(dispatch.T, normed, preferred_element_type=jnp.float32)
    outgoing = outgoing.astype(jnp.bfloat16).reshape(experts, capacity, width)
    combine = jnp.sum(jnp.where(hit, gates[:, :, None], 0.0), axis=1)
    combine_hi = combine.astype(jnp.bfloat16)
    combine_lo = (combine - combine_hi.astype(jnp.float32)).astype(jnp.bfloat16)
    local_in = expert_in[0]
    local_out = expert_out_w[0]
    arrived = lax.all_to_all(outgoing, "expert", split_axis=0, concat_axis=0, tiled=True)
    flat_rows = arrived.reshape(-1, width)
    returned = lax.all_to_all(
        swiglu_rows(flat_rows, local_in, local_out).astype(jnp.bfloat16).reshape(arrived.shape),
        "expert",
        split_axis=0,
        concat_axis=0,
        tiled=True,
    )
    returned = returned.reshape(slots, width)
    routed = jnp.dot(combine_hi, returned, preferred_element_type=jnp.float32)
    routed = routed + jnp.dot(combine_lo, returned, preferred_element_type=jnp.float32)
    shared_hidden = shared_out.shape[0]
    shared_mid = jnp.dot(
        normed,
        lax.all_gather(shared_in, "group", axis=0, tiled=True),
        preferred_element_type=jnp.float32,
    )
    shared_act = (
        jax.nn.silu(shared_mid[:, :shared_hidden]) * shared_mid[:, shared_hidden:]
    ).astype(jnp.bfloat16)
    shared_y = jnp.dot(
        shared_act,
        lax.all_gather(shared_out, "group", axis=1, tiled=True),
        preferred_element_type=jnp.float32,
    )
    return (hidden_f + shared_y + routed).astype(jnp.bfloat16)


def solution(mesh):
    placed = (
        P(("group", "expert"), None),
        P(("group", "expert"), None),
        P("group", None),
        P(),
        P(),
        P("group", None),
        P(None, "group"),
        P("expert", None, None),
        P("expert", None, None),
        P(("group", "expert"), None),
    )
    return jax.shard_map(
        per_device,
        mesh=mesh,
        in_specs=placed,
        out_specs=P(("group", "expert"), None),
        check_vma=False,
    )
```

```python
import jax
import jax.numpy as jnp
from jax import lax
from jax.sharding import PartitionSpec as P


def swiglu_rows(rows, w_in, w_out):
    width = w_out.shape[0]
    mid = jnp.dot(rows, w_in, preferred_element_type=jnp.float32)
    act = (jax.nn.silu(mid[:, :width]) * mid[:, width:]).astype(jnp.bfloat16)
    return jnp.dot(act, w_out, preferred_element_type=jnp.float32)


def per_device(
    context,
    residual,
    attn_out_w,
    norm_gain,
    router_w,
    shared_in,
    shared_out,
    expert_in,
    expert_out_w,
    routes,
):
    tok_rows = residual.shape[0]
    width = residual.shape[1]
    picks = routes.shape[1]
    experts = lax.axis_size("expert")
    capacity = 4 * tok_rows * picks // (3 * experts)
    slots = experts * capacity
    piece = attn_out_w.shape[1] // experts
    mine = lax.dynamic_slice_in_dim(attn_out_w, lax.axis_index("expert") * piece, piece, axis=1)
    mine = lax.all_gather(mine, "group", axis=0, tiled=True)
    attn = jnp.dot(
        context,
        lax.all_gather(mine, "expert", axis=1, tiled=True),
        preferred_element_type=jnp.float32,
    )
    hidden_state = (residual.astype(jnp.float32) + attn).astype(jnp.bfloat16)
    hidden_f = hidden_state.astype(jnp.float32)
    scale = lax.rsqrt(jnp.mean(hidden_f * hidden_f, axis=-1, keepdims=True) + 1e-06)
    normed = (hidden_f * scale * norm_gain).astype(jnp.bfloat16)
    logits = jnp.dot(normed, router_w, preferred_element_type=jnp.float32)
    chosen = routes[:, :, None] == jnp.arange(experts, dtype=jnp.int32)[None, None, :]
    picked = jnp.sum(jnp.where(chosen, logits[:, None, :], 0.0), axis=-1)
    sig = jax.nn.sigmoid(picked)
    gates = sig / jnp.sum(sig, axis=1, keepdims=True)
    flat_e = routes.reshape(-1)
    onehot = (flat_e[:, None] == jnp.arange(experts, dtype=jnp.int32)[None, :]).astype(jnp.int32)
    rank = jnp.cumsum(onehot, axis=0) - onehot
    position = jnp.sum(rank * onehot, axis=1)
    slot_of = (flat_e * capacity + position).reshape(tok_rows, picks)
    hit = slot_of[:, :, None] == jnp.arange(slots, dtype=jnp.int32)[None, None, :]
    dispatch = jnp.any(hit, axis=1).astype(jnp.bfloat16)
    outgoing = jnp.dot(dispatch.T, normed, preferred_element_type=jnp.float32)
    outgoing = outgoing.astype(jnp.bfloat16).reshape(experts, capacity, width)
    combine = jnp.sum(jnp.where(hit, gates[:, :, None], 0.0), axis=1)
    combine_hi = combine.astype(jnp.bfloat16)
    combine_lo = (combine - combine_hi.astype(jnp.float32)).astype(jnp.bfloat16)
    local_in = expert_in[0]
    local_out = expert_out_w[0]
    arrived = lax.all_to_all(outgoing, "expert", split_axis=0, concat_axis=0, tiled=True)
    flat_rows = arrived.reshape(-1, width)
    returned = lax.all_to_all(
        swiglu_rows(flat_rows, local_in, local_out).astype(jnp.bfloat16).reshape(arrived.shape),
        "expert",
        split_axis=0,
        concat_axis=0,
        tiled=True,
    )
    returned = returned.reshape(slots, width)
    routed = jnp.dot(combine_hi, returned, preferred_element_type=jnp.float32)
    routed = routed + jnp.dot(combine_lo, returned, preferred_element_type=jnp.float32)
    shared_hidden = shared_out.shape[0]
    shared_mid = jnp.dot(
        normed,
        lax.all_gather(shared_in, "group", axis=0, tiled=True),
        preferred_element_type=jnp.float32,
    )
    shared_act = (
        jax.nn.silu(shared_mid[:, :shared_hidden]) * shared_mid[:, shared_hidden:]
    ).astype(jnp.bfloat16)
    shared_y = jnp.dot(
        shared_act,
        lax.all_gather(shared_out, "group", axis=1, tiled=True),
        preferred_element_type=jnp.float32,
    )
    return (hidden_f + shared_y + routed).astype(jnp.bfloat16)


def solution(mesh):
    placed = (
        P(("group", "expert"), None),
        P(("group", "expert"), None),
        P("group", None),
        P(),
        P(),
        P("group", None),
        P(None, "group"),
        P("expert", None, None),
        P("expert", None, None),
        P(("group", "expert"), None),
    )
    return jax.shard_map(
        per_device,
        mesh=mesh,
        in_specs=placed,
        out_specs=P(("group", "expert"), None),
        check_vma=False,
    )
```

```python
import jax
import jax.numpy as jnp
from jax import lax
from jax.sharding import PartitionSpec as P


def swiglu_rows(rows, w_in, w_out):
    width = w_out.shape[0]
    mid = jnp.dot(rows, w_in, preferred_element_type=jnp.float32)
    act = (jax.nn.silu(mid[:, :width]) * mid[:, width:]).astype(jnp.bfloat16)
    return jnp.dot(act, w_out, preferred_element_type=jnp.float32)


def per_device(
    context,
    residual,
    attn_out_w,
    norm_gain,
    router_w,
    shared_in,
    shared_out,
    expert_in,
    expert_out_w,
    routes,
):
    tok_rows = residual.shape[0]
    width = residual.shape[1]
    picks = routes.shape[1]
    experts = lax.axis_size("expert")
    capacity = 4 * tok_rows * picks // (3 * experts)
    slots = experts * capacity
    attn = jnp.dot(
        context,
        lax.all_gather(attn_out_w, "group", axis=0, tiled=True),
        preferred_element_type=jnp.float32,
    )
    hidden_state = (residual.astype(jnp.float32) + attn).astype(jnp.bfloat16)
    hidden_f = hidden_state.astype(jnp.float32)
    scale = lax.rsqrt(jnp.mean(hidden_f * hidden_f, axis=-1, keepdims=True) + 1e-06)
    normed = (hidden_f * scale * norm_gain).astype(jnp.bfloat16)
    logits = jnp.dot(normed, router_w, preferred_element_type=jnp.float32)
    chosen = routes[:, :, None] == jnp.arange(experts, dtype=jnp.int32)[None, None, :]
    picked = jnp.sum(jnp.where(chosen, logits[:, None, :], 0.0), axis=-1)
    sig = jax.nn.sigmoid(picked)
    gates = sig / jnp.sum(sig, axis=1, keepdims=True)
    flat_e = routes.reshape(-1)
    onehot = (flat_e[:, None] == jnp.arange(experts, dtype=jnp.int32)[None, :]).astype(jnp.int32)
    rank = jnp.cumsum(onehot, axis=0) - onehot
    position = jnp.sum(rank * onehot, axis=1)
    slot_of = (flat_e * capacity + position).reshape(tok_rows, picks)
    hit = slot_of[:, :, None] == jnp.arange(slots, dtype=jnp.int32)[None, None, :]
    dispatch = jnp.any(hit, axis=1).astype(jnp.bfloat16)
    outgoing = jnp.dot(dispatch.T, normed, preferred_element_type=jnp.float32)
    outgoing = outgoing.astype(jnp.bfloat16).reshape(experts, capacity, width)
    combine = jnp.sum(jnp.where(hit, gates[:, :, None], 0.0), axis=1)
    combine_hi = combine.astype(jnp.bfloat16)
    combine_lo = (combine - combine_hi.astype(jnp.float32)).astype(jnp.bfloat16)
    local_in = expert_in[0]
    local_out = expert_out_w[0]
    chunks = 2
    part = capacity // chunks
    outgoing = outgoing.reshape(experts, chunks, part, width)
    combine_hi = combine_hi.reshape(tok_rows, experts, chunks, part)
    combine_lo = combine_lo.reshape(tok_rows, experts, chunks, part)
    routed = None
    for c in range(chunks):
        arrived = lax.all_to_all(outgoing[:, c], "expert", split_axis=0, concat_axis=0, tiled=True)
        done = swiglu_rows(arrived.reshape(-1, width), local_in, local_out).astype(jnp.bfloat16)
        returned = lax.all_to_all(
            done.reshape(arrived.shape), "expert", split_axis=0, concat_axis=0, tiled=True
        ).reshape(experts * part, width)
        hi = combine_hi[:, :, c].reshape(tok_rows, experts * part)
        lo = combine_lo[:, :, c].reshape(tok_rows, experts * part)
        step = jnp.dot(hi, returned, preferred_element_type=jnp.float32)
        step = step + jnp.dot(lo, returned, preferred_element_type=jnp.float32)
        routed = step if routed is None else routed + step
    shared_hidden = shared_out.shape[0]
    shared_mid = jnp.dot(
        normed,
        lax.all_gather(shared_in, "group", axis=0, tiled=True),
        preferred_element_type=jnp.float32,
    )
    shared_act = (
        jax.nn.silu(shared_mid[:, :shared_hidden]) * shared_mid[:, shared_hidden:]
    ).astype(jnp.bfloat16)
    shared_y = jnp.dot(
        shared_act,
        lax.all_gather(shared_out, "group", axis=1, tiled=True),
        preferred_element_type=jnp.float32,
    )
    return (hidden_f + shared_y + routed).astype(jnp.bfloat16)


def solution(mesh):
    placed = (
        P(("group", "expert"), None),
        P(("group", "expert"), None),
        P("group", None),
        P(),
        P(),
        P("group", None),
        P(None, "group"),
        P("expert", None, None),
        P("expert", None, None),
        P(("group", "expert"), None),
    )
    return jax.shard_map(
        per_device,
        mesh=mesh,
        in_specs=placed,
        out_specs=P(("group", "expert"), None),
        check_vma=False,
    )
```

```python
import jax
import jax.numpy as jnp
from jax import lax
from jax.sharding import PartitionSpec as P


def swiglu_rows(rows, w_in, w_out):
    width = w_out.shape[0]
    mid = jnp.dot(rows, w_in, preferred_element_type=jnp.float32)
    act = (jax.nn.silu(mid[:, :width]) * mid[:, width:]).astype(jnp.bfloat16)
    return jnp.dot(act, w_out, preferred_element_type=jnp.float32)


def gather_rows_by_chip(w):
    groups = lax.axis_size("group")
    ring = groups // 2
    g = lax.axis_index("group")
    y, c = g // 2, g % 2
    shifts = [0] + sorted(range(1, ring), key=lambda s: min(s, ring - s))
    got = [w]
    for s in shifts[1:]:
        pairs = [(2 * q + k, 2 * ((q + s) % ring) + k) for q in range(ring) for k in range(2)]
        got.append(lax.ppermute(w, "group", pairs))
    mine = jnp.stack(got)
    sib = lax.ppermute(mine, "group", [(i, i ^ 1) for i in range(groups)])
    order = [2 * ((y - s) % ring) + c for s in shifts] + [2 * ((y - s) % ring) + 1 - c for s in shifts]
    return jnp.concatenate([mine, sib]).reshape(-1, w.shape[1]), order


def per_device(
    context,
    residual,
    attn_out_w,
    norm_gain,
    router_w,
    shared_in,
    shared_out,
    expert_in,
    expert_out_w,
    routes,
):
    tok_rows = residual.shape[0]
    width = residual.shape[1]
    picks = routes.shape[1]
    experts = lax.axis_size("expert")
    capacity = 4 * tok_rows * picks // (3 * experts)
    slots = experts * capacity
    w_perm, order = gather_rows_by_chip(attn_out_w)
    block = attn_out_w.shape[0]
    ctx_perm = jnp.concatenate(
        [lax.dynamic_slice_in_dim(context, b * block, block, axis=1) for b in order], axis=1
    )
    attn = jnp.dot(ctx_perm, w_perm, preferred_element_type=jnp.float32)
    hidden_state = (residual.astype(jnp.float32) + attn).astype(jnp.bfloat16)
    hidden_f = hidden_state.astype(jnp.float32)
    scale = lax.rsqrt(jnp.mean(hidden_f * hidden_f, axis=-1, keepdims=True) + 1e-06)
    normed = (hidden_f * scale * norm_gain).astype(jnp.bfloat16)
    logits = jnp.dot(normed, router_w, preferred_element_type=jnp.float32)
    chosen = routes[:, :, None] == jnp.arange(experts, dtype=jnp.int32)[None, None, :]
    picked = jnp.sum(jnp.where(chosen, logits[:, None, :], 0.0), axis=-1)
    sig = jax.nn.sigmoid(picked)
    gates = sig / jnp.sum(sig, axis=1, keepdims=True)
    flat_e = routes.reshape(-1)
    onehot = (flat_e[:, None] == jnp.arange(experts, dtype=jnp.int32)[None, :]).astype(jnp.int32)
    rank = jnp.cumsum(onehot, axis=0) - onehot
    position = jnp.sum(rank * onehot, axis=1)
    slot_of = (flat_e * capacity + position).reshape(tok_rows, picks)
    hit = slot_of[:, :, None] == jnp.arange(slots, dtype=jnp.int32)[None, None, :]
    dispatch = jnp.any(hit, axis=1).astype(jnp.bfloat16)
    outgoing = jnp.dot(dispatch.T, normed, preferred_element_type=jnp.float32)
    outgoing = outgoing.astype(jnp.bfloat16).reshape(experts, capacity, width)
    combine = jnp.sum(jnp.where(hit, gates[:, :, None], 0.0), axis=1)
    combine_hi = combine.astype(jnp.bfloat16)
    combine_lo = (combine - combine_hi.astype(jnp.float32)).astype(jnp.bfloat16)
    local_in = expert_in[0]
    local_out = expert_out_w[0]
    arrived = lax.all_to_all(outgoing, "expert", split_axis=0, concat_axis=0, tiled=True)
    flat_rows = arrived.reshape(-1, width)
    returned = lax.all_to_all(
        swiglu_rows(flat_rows, local_in, local_out).astype(jnp.bfloat16).reshape(arrived.shape),
        "expert",
        split_axis=0,
        concat_axis=0,
        tiled=True,
    )
    returned = returned.reshape(slots, width)
    routed = jnp.dot(combine_hi, returned, preferred_element_type=jnp.float32)
    routed = routed + jnp.dot(combine_lo, returned, preferred_element_type=jnp.float32)
    shared_hidden = shared_out.shape[0]
    shared_mid = jnp.dot(
        normed,
        lax.all_gather(shared_in, "group", axis=0, tiled=True),
        preferred_element_type=jnp.float32,
    )
    shared_act = (
        jax.nn.silu(shared_mid[:, :shared_hidden]) * shared_mid[:, shared_hidden:]
    ).astype(jnp.bfloat16)
    shared_y = jnp.dot(
        shared_act,
        lax.all_gather(shared_out, "group", axis=1, tiled=True),
        preferred_element_type=jnp.float32,
    )
    return (hidden_f + shared_y + routed).astype(jnp.bfloat16)


def solution(mesh):
    placed = (
        P(("group", "expert"), None),
        P(("group", "expert"), None),
        P("group", None),
        P(),
        P(),
        P("group", None),
        P(None, "group"),
        P("expert", None, None),
        P("expert", None, None),
        P(("group", "expert"), None),
    )
    return jax.shard_map(
        per_device,
        mesh=mesh,
        in_specs=placed,
        out_specs=P(("group", "expert"), None),
        check_vma=False,
    )
```

```python
import jax
import jax.numpy as jnp
from jax import lax
from jax.sharding import PartitionSpec as P


def swiglu_rows(rows, w_in, w_out):
    width = w_out.shape[0]
    mid = jnp.dot(rows, w_in, preferred_element_type=jnp.float32)
    act = (jax.nn.silu(mid[:, :width]) * mid[:, width:]).astype(jnp.bfloat16)
    return jnp.dot(act, w_out, preferred_element_type=jnp.float32)


def gather_rows_by_chip(w):
    groups = lax.axis_size("group")
    ring = groups // 2
    g = lax.axis_index("group")
    y, c = g // 2, g % 2
    shifts = [0] + sorted(range(1, ring), key=lambda s: min(s, ring - s))
    got = [w]
    for s in shifts[1:]:
        pairs = [(2 * q + k, 2 * ((q + s) % ring) + k) for q in range(ring) for k in range(2)]
        got.append(lax.ppermute(w, "group", pairs))
    mine = jnp.stack(got)
    sib = lax.ppermute(mine, "group", [(i, i ^ 1) for i in range(groups)])
    order = [2 * ((y - s) % ring) + c for s in shifts] + [2 * ((y - s) % ring) + 1 - c for s in shifts]
    return jnp.concatenate([mine, sib]).reshape(-1, w.shape[1]), order


def per_device(
    context,
    residual,
    attn_out_w,
    norm_gain,
    router_w,
    shared_in,
    shared_out,
    expert_in,
    expert_out_w,
    routes,
):
    tok_rows = residual.shape[0]
    width = residual.shape[1]
    picks = routes.shape[1]
    experts = lax.axis_size("expert")
    capacity = 4 * tok_rows * picks // (3 * experts)
    slots = experts * capacity
    w_perm, order = gather_rows_by_chip(attn_out_w)
    w_perm, shared_in, shared_out = lax.optimization_barrier((w_perm, shared_in, shared_out))
    shared_in = lax.all_gather(shared_in, "group", axis=0, tiled=True)
    shared_out = lax.all_gather(shared_out, "group", axis=1, tiled=True)
    block = attn_out_w.shape[0]
    ctx_perm = jnp.concatenate(
        [lax.dynamic_slice_in_dim(context, b * block, block, axis=1) for b in order], axis=1
    )
    attn = jnp.dot(ctx_perm, w_perm, preferred_element_type=jnp.float32)
    hidden_state = (residual.astype(jnp.float32) + attn).astype(jnp.bfloat16)
    hidden_f = hidden_state.astype(jnp.float32)
    scale = lax.rsqrt(jnp.mean(hidden_f * hidden_f, axis=-1, keepdims=True) + 1e-06)
    normed = (hidden_f * scale * norm_gain).astype(jnp.bfloat16)
    logits = jnp.dot(normed, router_w, preferred_element_type=jnp.float32)
    chosen = routes[:, :, None] == jnp.arange(experts, dtype=jnp.int32)[None, None, :]
    picked = jnp.sum(jnp.where(chosen, logits[:, None, :], 0.0), axis=-1)
    sig = jax.nn.sigmoid(picked)
    gates = sig / jnp.sum(sig, axis=1, keepdims=True)
    flat_e = routes.reshape(-1)
    onehot = (flat_e[:, None] == jnp.arange(experts, dtype=jnp.int32)[None, :]).astype(jnp.int32)
    rank = jnp.cumsum(onehot, axis=0) - onehot
    position = jnp.sum(rank * onehot, axis=1)
    slot_of = (flat_e * capacity + position).reshape(tok_rows, picks)
    hit = slot_of[:, :, None] == jnp.arange(slots, dtype=jnp.int32)[None, None, :]
    dispatch = jnp.any(hit, axis=1).astype(jnp.bfloat16)
    outgoing = jnp.dot(dispatch.T, normed, preferred_element_type=jnp.float32)
    outgoing = outgoing.astype(jnp.bfloat16).reshape(experts, capacity, width)
    combine = jnp.sum(jnp.where(hit, gates[:, :, None], 0.0), axis=1)
    combine_hi = combine.astype(jnp.bfloat16)
    combine_lo = (combine - combine_hi.astype(jnp.float32)).astype(jnp.bfloat16)
    local_in = expert_in[0]
    local_out = expert_out_w[0]
    arrived = lax.all_to_all(outgoing, "expert", split_axis=0, concat_axis=0, tiled=True)
    flat_rows = arrived.reshape(-1, width)
    expert_rows = swiglu_rows(flat_rows, local_in, local_out).astype(jnp.bfloat16)
    expert_rows, shared_in, shared_out = lax.optimization_barrier((expert_rows, shared_in, shared_out))
    returned = lax.all_to_all(
        expert_rows.reshape(arrived.shape),
        "expert",
        split_axis=0,
        concat_axis=0,
        tiled=True,
    )
    returned = returned.reshape(slots, width)
    routed = jnp.dot(combine_hi, returned, preferred_element_type=jnp.float32)
    routed = routed + jnp.dot(combine_lo, returned, preferred_element_type=jnp.float32)
    shared_hidden = shared_out.shape[0]
    shared_mid = jnp.dot(
        normed,
        shared_in,
        preferred_element_type=jnp.float32,
    )
    shared_act = (
        jax.nn.silu(shared_mid[:, :shared_hidden]) * shared_mid[:, shared_hidden:]
    ).astype(jnp.bfloat16)
    shared_y = jnp.dot(
        shared_act,
        shared_out,
        preferred_element_type=jnp.float32,
    )
    return (hidden_f + shared_y + routed).astype(jnp.bfloat16)


def solution(mesh):
    placed = (
        P(("group", "expert"), None),
        P(("group", "expert"), None),
        P("group", None),
        P(),
        P(),
        P("group", None),
        P(None, "group"),
        P("expert", None, None),
        P("expert", None, None),
        P(("group", "expert"), None),
    )
    return jax.shard_map(
        per_device,
        mesh=mesh,
        in_specs=placed,
        out_specs=P(("group", "expert"), None),
        check_vma=False,
    )
```

```python
import jax
import jax.numpy as jnp
from jax import lax
from jax.sharding import PartitionSpec as P


def swiglu_rows(rows, w_in, w_out):
    width = w_out.shape[0]
    mid = jnp.dot(rows, w_in, preferred_element_type=jnp.float32)
    act = (jax.nn.silu(mid[:, :width]) * mid[:, width:]).astype(jnp.bfloat16)
    return jnp.dot(act, w_out, preferred_element_type=jnp.float32)


def gather_rows_by_chip(w):
    groups = lax.axis_size("group")
    ring = groups // 2
    g = lax.axis_index("group")
    y, c = g // 2, g % 2

    def shift(x, s):
        pairs = [(2 * q + k, 2 * ((q + s) % ring) + k) for q in range(ring) for k in range(2)]
        return lax.ppermute(x, "group", pairs)

    def sib(x):
        return lax.ppermute(x, "group", [(i, i ^ 1) for i in range(groups)])

    half = w.shape[0] // 2
    from_left = shift(w, 1)
    from_right = shift(w, -1)
    far = jnp.concatenate(
        [shift(from_right[:half], -1), shift(from_left[half:], 1)], axis=0
    )
    pieces = [w, from_left, from_right, far, sib(w), sib(from_left), sib(from_right), sib(far)]
    ys = [y, y - 1, y + 1, y + 2]
    order = [2 * (q % ring) + c for q in ys] + [2 * (q % ring) + 1 - c for q in ys]
    return pieces, order


def per_device(
    context,
    residual,
    attn_out_w,
    norm_gain,
    router_w,
    shared_in,
    shared_out,
    expert_in,
    expert_out_w,
    routes,
):
    tok_rows = residual.shape[0]
    width = residual.shape[1]
    picks = routes.shape[1]
    experts = lax.axis_size("expert")
    capacity = 4 * tok_rows * picks // (3 * experts)
    slots = experts * capacity
    if lax.axis_size("group") == 8:
        pieces, order = gather_rows_by_chip(attn_out_w)
    else:
        pieces = [lax.all_gather(attn_out_w, "group", axis=0, tiled=True)]
        order = [0]
    pieces, shared_in, shared_out = lax.optimization_barrier((pieces, shared_in, shared_out))
    shared_in = lax.all_gather(shared_in, "group", axis=0, tiled=True)
    shared_out = lax.all_gather(shared_out, "group", axis=1, tiled=True)
    block = pieces[0].shape[0]
    ctx_blocks = context.reshape(tok_rows, -1, block)
    ctx_perm = jnp.take(ctx_blocks, jnp.stack(order), axis=1)
    attn = None
    for i, piece in enumerate(pieces):
        term = jnp.dot(ctx_perm[:, i, :], piece, preferred_element_type=jnp.float32)
        attn = term if attn is None else attn + term
    hidden_state = (residual.astype(jnp.float32) + attn).astype(jnp.bfloat16)
    hidden_f = hidden_state.astype(jnp.float32)
    scale = lax.rsqrt(jnp.mean(hidden_f * hidden_f, axis=-1, keepdims=True) + 1e-06)
    normed = (hidden_f * scale * norm_gain).astype(jnp.bfloat16)
    logits = jnp.dot(normed, router_w, preferred_element_type=jnp.float32)
    chosen = routes[:, :, None] == jnp.arange(experts, dtype=jnp.int32)[None, None, :]
    picked = jnp.sum(jnp.where(chosen, logits[:, None, :], 0.0), axis=-1)
    sig = jax.nn.sigmoid(picked)
    gates = sig / jnp.sum(sig, axis=1, keepdims=True)
    flat_e = routes.reshape(-1)
    onehot = (flat_e[:, None] == jnp.arange(experts, dtype=jnp.int32)[None, :]).astype(jnp.int32)
    rank = jnp.cumsum(onehot, axis=0) - onehot
    position = jnp.sum(rank * onehot, axis=1)
    slot_of = (flat_e * capacity + position).reshape(tok_rows, picks)
    hit = slot_of[:, :, None] == jnp.arange(slots, dtype=jnp.int32)[None, None, :]
    dispatch = jnp.any(hit, axis=1).astype(jnp.bfloat16)
    outgoing = jnp.dot(dispatch.T, normed, preferred_element_type=jnp.float32)
    outgoing = outgoing.astype(jnp.bfloat16).reshape(experts, capacity, width)
    combine = jnp.sum(jnp.where(hit, gates[:, :, None], 0.0), axis=1)
    combine_hi = combine.astype(jnp.bfloat16)
    combine_lo = (combine - combine_hi.astype(jnp.float32)).astype(jnp.bfloat16)
    local_in = expert_in[0]
    local_out = expert_out_w[0]
    arrived = lax.all_to_all(outgoing, "expert", split_axis=0, concat_axis=0, tiled=True)
    flat_rows = arrived.reshape(-1, width)
    expert_rows = swiglu_rows(flat_rows, local_in, local_out).astype(jnp.bfloat16)
    expert_rows, shared_in, shared_out = lax.optimization_barrier((expert_rows, shared_in, shared_out))
    returned = lax.all_to_all(
        expert_rows.reshape(arrived.shape),
        "expert",
        split_axis=0,
        concat_axis=0,
        tiled=True,
    )
    returned = returned.reshape(slots, width)
    routed = jnp.dot(combine_hi, returned, preferred_element_type=jnp.float32)
    routed = routed + jnp.dot(combine_lo, returned, preferred_element_type=jnp.float32)
    shared_hidden = shared_out.shape[0]
    shared_mid = jnp.dot(
        normed,
        shared_in,
        preferred_element_type=jnp.float32,
    )
    shared_act = (
        jax.nn.silu(shared_mid[:, :shared_hidden]) * shared_mid[:, shared_hidden:]
    ).astype(jnp.bfloat16)
    shared_y = jnp.dot(
        shared_act,
        shared_out,
        preferred_element_type=jnp.float32,
    )
    return (hidden_f + shared_y + routed).astype(jnp.bfloat16)


def solution(mesh):
    placed = (
        P(("group", "expert"), None),
        P(("group", "expert"), None),
        P("group", None),
        P(),
        P(),
        P("group", None),
        P(None, "group"),
        P("expert", None, None),
        P("expert", None, None),
        P(("group", "expert"), None),
    )
    return jax.shard_map(
        per_device,
        mesh=mesh,
        in_specs=placed,
        out_specs=P(("group", "expert"), None),
        check_vma=False,
    )
```

```python
import jax
import jax.numpy as jnp
from jax import lax
from jax.sharding import PartitionSpec as P


def swiglu_rows(rows, w_in, w_out):
    width = w_out.shape[0]
    mid = jnp.dot(rows, w_in, preferred_element_type=jnp.float32)
    act = (jax.nn.silu(mid[:, :width]) * mid[:, width:]).astype(jnp.bfloat16)
    return jnp.dot(act, w_out, preferred_element_type=jnp.float32)


def gather_rows_by_chip(w, passenger):
    groups = lax.axis_size("group")
    ring = groups // 2
    g = lax.axis_index("group")
    y, c = g // 2, g % 2

    def shift(x, s):
        pairs = [(2 * q + k, 2 * ((q + s) % ring) + k) for q in range(ring) for k in range(2)]
        return lax.ppermute(x, "group", pairs)

    def sib(x):
        return lax.ppermute(x, "group", [(i, i ^ 1) for i in range(groups)])

    half = w.shape[0] // 2
    from_left = shift(w, 1)
    from_right = shift(w, -1)
    from_left, passenger = lax.optimization_barrier((from_left, passenger))
    far = jnp.concatenate(
        [shift(from_right[:half], -1), shift(from_left[half:], 1)], axis=0
    )
    pieces = [w, from_left, from_right, far, sib(w), sib(from_left), sib(from_right), sib(far)]
    return pieces, passenger


def chip_gather_order():
    ring = lax.axis_size("group") // 2
    g = lax.axis_index("group")
    y, c = g // 2, g % 2
    ys = (y + jnp.array([0, -1, 1, 2], jnp.int32) + ring) % ring
    return jnp.concatenate([2 * ys + c, 2 * ys + 1 - c])


def per_device(
    context,
    residual,
    attn_out_w,
    norm_gain,
    router_w,
    shared_in,
    shared_out,
    expert_in,
    expert_out_w,
    routes,
):
    tok_rows = residual.shape[0]
    width = residual.shape[1]
    picks = routes.shape[1]
    experts = lax.axis_size("expert")
    capacity = 4 * tok_rows * picks // (3 * experts)
    slots = experts * capacity
    flat_e = routes.reshape(-1)
    onehot = (flat_e[:, None] == jnp.arange(experts, dtype=jnp.int32)[None, :]).astype(jnp.int32)
    rank = jnp.cumsum(onehot, axis=0) - onehot
    position = jnp.sum(rank * onehot, axis=1)
    slot_of = (flat_e * capacity + position).reshape(tok_rows, picks)
    hit = slot_of[:, :, None] == jnp.arange(slots, dtype=jnp.int32)[None, None, :]
    dispatch = jnp.any(hit, axis=1).astype(jnp.bfloat16)
    block = attn_out_w.shape[0]
    ctx_blocks = context.reshape(tok_rows, -1, block)
    groups = lax.axis_size("group")
    if groups == 8:
        own = lax.axis_index("group")
        first = jnp.dot(
            lax.dynamic_index_in_dim(ctx_blocks, own, 1, keepdims=False),
            attn_out_w,
            preferred_element_type=jnp.float32,
        )
        ctx_perm = jnp.take(ctx_blocks, chip_gather_order(), axis=1)
        pieces, (slot_of, dispatch, first, ctx_perm) = gather_rows_by_chip(
            attn_out_w, (slot_of, dispatch, first, ctx_perm)
        )
    else:
        pieces = [lax.all_gather(attn_out_w, "group", axis=0, tiled=True)]
        ctx_perm = context[:, None, :]
        first = None
    pieces, shared_in, shared_out = lax.optimization_barrier((pieces, shared_in, shared_out))
    shared_in = lax.all_gather(shared_in, "group", axis=0, tiled=True)
    shared_out = lax.all_gather(shared_out, "group", axis=1, tiled=True)
    attn = first
    for i, piece in enumerate(pieces):
        if first is not None and i == 0:
            continue
        term = jnp.dot(ctx_perm[:, i, :], piece, preferred_element_type=jnp.float32)
        attn = term if attn is None else attn + term
    hidden_state = (residual.astype(jnp.float32) + attn).astype(jnp.bfloat16)
    hidden_f = hidden_state.astype(jnp.float32)
    scale = lax.rsqrt(jnp.mean(hidden_f * hidden_f, axis=-1, keepdims=True) + 1e-06)
    normed = (hidden_f * scale * norm_gain).astype(jnp.bfloat16)
    logits = jnp.dot(normed, router_w, preferred_element_type=jnp.float32)
    chosen = routes[:, :, None] == jnp.arange(experts, dtype=jnp.int32)[None, None, :]
    picked = jnp.sum(jnp.where(chosen, logits[:, None, :], 0.0), axis=-1)
    sig = jax.nn.sigmoid(picked)
    gates = sig / jnp.sum(sig, axis=1, keepdims=True)
    outgoing = jnp.dot(dispatch.T, normed, preferred_element_type=jnp.float32)
    outgoing = outgoing.astype(jnp.bfloat16).reshape(experts, capacity, width)
    hit = slot_of[:, :, None] == jnp.arange(slots, dtype=jnp.int32)[None, None, :]
    combine = jnp.sum(jnp.where(hit, gates[:, :, None], 0.0), axis=1)
    combine_hi = combine.astype(jnp.bfloat16)
    combine_lo = (combine - combine_hi.astype(jnp.float32)).astype(jnp.bfloat16)
    local_in = expert_in[0]
    local_out = expert_out_w[0]
    arrived = lax.all_to_all(outgoing, "expert", split_axis=0, concat_axis=0, tiled=True)
    flat_rows = arrived.reshape(-1, width)
    expert_rows = swiglu_rows(flat_rows, local_in, local_out).astype(jnp.bfloat16)
    expert_rows, shared_in, shared_out = lax.optimization_barrier((expert_rows, shared_in, shared_out))
    returned = lax.all_to_all(
        expert_rows.reshape(arrived.shape),
        "expert",
        split_axis=0,
        concat_axis=0,
        tiled=True,
    )
    returned = returned.reshape(slots, width)
    routed = jnp.dot(combine_hi, returned, preferred_element_type=jnp.float32)
    routed = routed + jnp.dot(combine_lo, returned, preferred_element_type=jnp.float32)
    shared_hidden = shared_out.shape[0]
    shared_mid = jnp.dot(
        normed,
        shared_in,
        preferred_element_type=jnp.float32,
    )
    shared_act = (
        jax.nn.silu(shared_mid[:, :shared_hidden]) * shared_mid[:, shared_hidden:]
    ).astype(jnp.bfloat16)
    shared_y = jnp.dot(
        shared_act,
        shared_out,
        preferred_element_type=jnp.float32,
    )
    return (hidden_f + shared_y + routed).astype(jnp.bfloat16)


def solution(mesh):
    placed = (
        P(("group", "expert"), None),
        P(("group", "expert"), None),
        P("group", None),
        P(),
        P(),
        P("group", None),
        P(None, "group"),
        P("expert", None, None),
        P("expert", None, None),
        P(("group", "expert"), None),
    )
    return jax.shard_map(
        per_device,
        mesh=mesh,
        in_specs=placed,
        out_specs=P(("group", "expert"), None),
        check_vma=False,
    )
```

```python
import jax
import jax.numpy as jnp
from jax import lax
from jax.sharding import PartitionSpec as P


def swiglu_rows(rows, w_in, w_out):
    width = w_out.shape[0]
    mid = jnp.dot(rows, w_in, preferred_element_type=jnp.float32)
    act = (jax.nn.silu(mid[:, :width]) * mid[:, width:]).astype(jnp.bfloat16)
    return jnp.dot(act, w_out, preferred_element_type=jnp.float32)


def gather_rows_by_chip(w, passenger):
    groups = lax.axis_size("group")
    ring = groups // 2
    g = lax.axis_index("group")
    y, c = g // 2, g % 2

    def shift(x, s):
        pairs = [(2 * q + k, 2 * ((q + s) % ring) + k) for q in range(ring) for k in range(2)]
        return lax.ppermute(x, "group", pairs)

    def sib(x):
        return lax.ppermute(x, "group", [(i, i ^ 1) for i in range(groups)])

    half = w.shape[0] // 2
    from_left = shift(w, 1)
    from_right = shift(w, -1)
    from_left, passenger = lax.optimization_barrier((from_left, passenger))
    far = jnp.concatenate(
        [shift(from_right[:half], -1), shift(from_left[half:], 1)], axis=0
    )
    pieces = [w, from_left, from_right, far, sib(w), sib(from_left), sib(from_right), sib(far)]
    return pieces, passenger


def chip_gather_order():
    ring = lax.axis_size("group") // 2
    g = lax.axis_index("group")
    y, c = g // 2, g % 2
    ys = (y + jnp.array([0, -1, 1, 2], jnp.int32) + ring) % ring
    return jnp.concatenate([2 * ys + c, 2 * ys + 1 - c])


def per_device(
    context,
    residual,
    attn_out_w,
    norm_gain,
    router_w,
    shared_in,
    shared_out,
    expert_in,
    expert_out_w,
    routes,
):
    tok_rows = residual.shape[0]
    width = residual.shape[1]
    picks = routes.shape[1]
    experts = lax.axis_size("expert")
    capacity = 4 * tok_rows * picks // (3 * experts)
    slots = experts * capacity
    flat_e = routes.reshape(-1)
    onehot = (flat_e[:, None] == jnp.arange(experts, dtype=jnp.int32)[None, :]).astype(jnp.int32)
    rank = jnp.cumsum(onehot, axis=0) - onehot
    position = jnp.sum(rank * onehot, axis=1)
    slot_of = (flat_e * capacity + position).reshape(tok_rows, picks)
    hit = slot_of[:, :, None] == jnp.arange(slots, dtype=jnp.int32)[None, None, :]
    dispatch = jnp.any(hit, axis=1).astype(jnp.bfloat16)
    block = attn_out_w.shape[0]
    groups = lax.axis_size("group")
    if groups == 8:
        src = chip_gather_order()[:, None] * block + jnp.arange(block, dtype=jnp.int32)[None, :]
        perm = (jnp.arange(context.shape[1], dtype=jnp.int32)[:, None] == src.reshape(1, -1))
        ctx_perm = jnp.dot(context, perm.astype(jnp.bfloat16), preferred_element_type=jnp.float32)
        ctx_perm = ctx_perm.astype(jnp.bfloat16).reshape(tok_rows, groups, block)
        pieces, (slot_of, dispatch, ctx_perm) = gather_rows_by_chip(
            attn_out_w, (slot_of, dispatch, ctx_perm)
        )
    else:
        pieces = [lax.all_gather(attn_out_w, "group", axis=0, tiled=True)]
        ctx_perm = context[:, None, :]
    pieces, shared_in, shared_out = lax.optimization_barrier((pieces, shared_in, shared_out))
    shared_in = lax.all_gather(shared_in, "group", axis=0, tiled=True)
    shared_out = lax.all_gather(shared_out, "group", axis=1, tiled=True)
    attn = None
    for i, piece in enumerate(pieces):
        term = jnp.dot(ctx_perm[:, i, :], piece, preferred_element_type=jnp.float32)
        attn = term if attn is None else attn + term
    hidden_state = (residual.astype(jnp.float32) + attn).astype(jnp.bfloat16)
    hidden_f = hidden_state.astype(jnp.float32)
    scale = lax.rsqrt(jnp.mean(hidden_f * hidden_f, axis=-1, keepdims=True) + 1e-06)
    normed = (hidden_f * scale * norm_gain).astype(jnp.bfloat16)
    logits = jnp.dot(normed, router_w, preferred_element_type=jnp.float32)
    chosen = routes[:, :, None] == jnp.arange(experts, dtype=jnp.int32)[None, None, :]
    picked = jnp.sum(jnp.where(chosen, logits[:, None, :], 0.0), axis=-1)
    sig = jax.nn.sigmoid(picked)
    gates = sig / jnp.sum(sig, axis=1, keepdims=True)
    outgoing = jnp.dot(dispatch.T, normed, preferred_element_type=jnp.float32)
    outgoing = outgoing.astype(jnp.bfloat16).reshape(experts, capacity, width)
    hit = slot_of[:, :, None] == jnp.arange(slots, dtype=jnp.int32)[None, None, :]
    combine = jnp.sum(jnp.where(hit, gates[:, :, None], 0.0), axis=1)
    combine_hi = combine.astype(jnp.bfloat16)
    combine_lo = (combine - combine_hi.astype(jnp.float32)).astype(jnp.bfloat16)
    local_in = expert_in[0]
    local_out = expert_out_w[0]
    arrived = lax.all_to_all(outgoing, "expert", split_axis=0, concat_axis=0, tiled=True)
    flat_rows = arrived.reshape(-1, width)
    expert_rows = swiglu_rows(flat_rows, local_in, local_out).astype(jnp.bfloat16)
    expert_rows, shared_in, shared_out = lax.optimization_barrier((expert_rows, shared_in, shared_out))
    returned = lax.all_to_all(
        expert_rows.reshape(arrived.shape),
        "expert",
        split_axis=0,
        concat_axis=0,
        tiled=True,
    )
    returned = returned.reshape(slots, width)
    routed = jnp.dot(combine_hi, returned, preferred_element_type=jnp.float32)
    routed = routed + jnp.dot(combine_lo, returned, preferred_element_type=jnp.float32)
    shared_hidden = shared_out.shape[0]
    shared_mid = jnp.dot(
        normed,
        shared_in,
        preferred_element_type=jnp.float32,
    )
    shared_act = (
        jax.nn.silu(shared_mid[:, :shared_hidden]) * shared_mid[:, shared_hidden:]
    ).astype(jnp.bfloat16)
    shared_y = jnp.dot(
        shared_act,
        shared_out,
        preferred_element_type=jnp.float32,
    )
    return (hidden_f + shared_y + routed).astype(jnp.bfloat16)


def solution(mesh):
    placed = (
        P(("group", "expert"), None),
        P(("group", "expert"), None),
        P("group", None),
        P(),
        P(),
        P("group", None),
        P(None, "group"),
        P("expert", None, None),
        P("expert", None, None),
        P(("group", "expert"), None),
    )
    return jax.shard_map(
        per_device,
        mesh=mesh,
        in_specs=placed,
        out_specs=P(("group", "expert"), None),
        check_vma=False,
    )
```

```python
import jax
import jax.numpy as jnp
from jax import lax
from jax.sharding import PartitionSpec as P


def swiglu_rows(rows, w_in, w_out):
    width = w_out.shape[0]
    mid = jnp.dot(rows, w_in, preferred_element_type=jnp.float32)
    act = (jax.nn.silu(mid[:, :width]) * mid[:, width:]).astype(jnp.bfloat16)
    return jnp.dot(act, w_out, preferred_element_type=jnp.float32)


def gather_rows_by_chip(w, passenger):
    groups = lax.axis_size("group")
    ring = groups // 2
    g = lax.axis_index("group")
    y, c = g // 2, g % 2

    def shift(x, s):
        pairs = [(2 * q + k, 2 * ((q + s) % ring) + k) for q in range(ring) for k in range(2)]
        return lax.ppermute(x, "group", pairs)

    def sib(x):
        return lax.ppermute(x, "group", [(i, i ^ 1) for i in range(groups)])

    half = w.shape[0] // 2
    from_left = shift(w, 1)
    from_right = shift(w, -1)
    from_left, passenger = lax.optimization_barrier((from_left, passenger))
    far = jnp.concatenate(
        [shift(from_right[:half], -1), shift(from_left[half:], 1)], axis=0
    )
    pieces = [w, from_left, from_right, far, sib(w), sib(from_left), sib(from_right), sib(far)]
    return pieces, passenger


def chip_gather_order():
    ring = lax.axis_size("group") // 2
    g = lax.axis_index("group")
    y, c = g // 2, g % 2
    ys = (y + jnp.array([0, -1, 1, 2], jnp.int32) + ring) % ring
    return jnp.concatenate([2 * ys + c, 2 * ys + 1 - c])


def per_device(
    context,
    residual,
    attn_out_w,
    norm_gain,
    router_w,
    shared_in,
    shared_out,
    expert_in,
    expert_out_w,
    routes,
):
    tok_rows = residual.shape[0]
    width = residual.shape[1]
    picks = routes.shape[1]
    experts = lax.axis_size("expert")
    capacity = 4 * tok_rows * picks // (3 * experts)
    slots = experts * capacity
    flat_e = routes.reshape(-1)
    onehot = (flat_e[:, None] == jnp.arange(experts, dtype=jnp.int32)[None, :]).astype(jnp.int32)
    rank = jnp.cumsum(onehot, axis=0) - onehot
    position = jnp.sum(rank * onehot, axis=1)
    slot_of = (flat_e * capacity + position).reshape(tok_rows, picks)
    hit = slot_of[:, :, None] == jnp.arange(slots, dtype=jnp.int32)[None, None, :]
    dispatch = jnp.any(hit, axis=1).astype(jnp.bfloat16)
    block = attn_out_w.shape[0]
    groups = lax.axis_size("group")
    if groups == 8:
        src = chip_gather_order()[:, None] * block + jnp.arange(block, dtype=jnp.int32)[None, :]
        perm = (jnp.arange(context.shape[1], dtype=jnp.int32)[:, None] == src.reshape(1, -1))
        ctx_perm = jnp.dot(context, perm.astype(jnp.bfloat16), preferred_element_type=jnp.float32)
        ctx_perm = ctx_perm.astype(jnp.bfloat16).reshape(tok_rows, groups, block)
        pieces, (slot_of, dispatch, ctx_perm) = gather_rows_by_chip(
            attn_out_w, (slot_of, dispatch, ctx_perm)
        )
    else:
        pieces = [lax.all_gather(attn_out_w, "group", axis=0, tiled=True)]
        ctx_perm = context[:, None, :]
    pieces, shared_in, shared_out = lax.optimization_barrier((pieces, shared_in, shared_out))
    shared_in = lax.all_gather(shared_in, "group", axis=0, tiled=True)
    shared_out = lax.all_gather(shared_out, "group", axis=1, tiled=True)
    attn = jnp.dot(
        ctx_perm.reshape(tok_rows, -1),
        jnp.concatenate(pieces, axis=0),
        preferred_element_type=jnp.float32,
    )
    hidden_state = (residual.astype(jnp.float32) + attn).astype(jnp.bfloat16)
    hidden_f = hidden_state.astype(jnp.float32)
    scale = lax.rsqrt(jnp.mean(hidden_f * hidden_f, axis=-1, keepdims=True) + 1e-06)
    normed = (hidden_f * scale * norm_gain).astype(jnp.bfloat16)
    logits = jnp.dot(normed, router_w, preferred_element_type=jnp.float32)
    chosen = routes[:, :, None] == jnp.arange(experts, dtype=jnp.int32)[None, None, :]
    picked = jnp.sum(jnp.where(chosen, logits[:, None, :], 0.0), axis=-1)
    sig = jax.nn.sigmoid(picked)
    gates = sig / jnp.sum(sig, axis=1, keepdims=True)
    outgoing = jnp.dot(dispatch.T, normed, preferred_element_type=jnp.float32)
    outgoing = outgoing.astype(jnp.bfloat16).reshape(experts, capacity, width)
    hit = slot_of[:, :, None] == jnp.arange(slots, dtype=jnp.int32)[None, None, :]
    combine = jnp.sum(jnp.where(hit, gates[:, :, None], 0.0), axis=1)
    combine_hi = combine.astype(jnp.bfloat16)
    combine_lo = (combine - combine_hi.astype(jnp.float32)).astype(jnp.bfloat16)
    local_in = expert_in[0]
    local_out = expert_out_w[0]
    arrived = lax.all_to_all(outgoing, "expert", split_axis=0, concat_axis=0, tiled=True)
    flat_rows = arrived.reshape(-1, width)
    expert_rows = swiglu_rows(flat_rows, local_in, local_out).astype(jnp.bfloat16)
    expert_rows, shared_in, shared_out = lax.optimization_barrier((expert_rows, shared_in, shared_out))
    returned = lax.all_to_all(
        expert_rows.reshape(arrived.shape),
        "expert",
        split_axis=0,
        concat_axis=0,
        tiled=True,
    )
    returned = returned.reshape(slots, width)
    routed = jnp.dot(combine_hi, returned, preferred_element_type=jnp.float32)
    routed = routed + jnp.dot(combine_lo, returned, preferred_element_type=jnp.float32)
    shared_hidden = shared_out.shape[0]
    shared_mid = jnp.dot(
        normed,
        shared_in,
        preferred_element_type=jnp.float32,
    )
    shared_act = (
        jax.nn.silu(shared_mid[:, :shared_hidden]) * shared_mid[:, shared_hidden:]
    ).astype(jnp.bfloat16)
    shared_y = jnp.dot(
        shared_act,
        shared_out,
        preferred_element_type=jnp.float32,
    )
    return (hidden_f + shared_y + routed).astype(jnp.bfloat16)


def solution(mesh):
    placed = (
        P(("group", "expert"), None),
        P(("group", "expert"), None),
        P("group", None),
        P(),
        P(),
        P("group", None),
        P(None, "group"),
        P("expert", None, None),
        P("expert", None, None),
        P(("group", "expert"), None),
    )
    return jax.shard_map(
        per_device,
        mesh=mesh,
        in_specs=placed,
        out_specs=P(("group", "expert"), None),
        check_vma=False,
    )
```

```python
import jax
import jax.numpy as jnp
from jax import lax
from jax.sharding import PartitionSpec as P
from jax.experimental import pallas as pl


def swiglu_rows(rows, w_in, w_out):
    width = w_out.shape[0]
    mid = jnp.dot(rows, w_in, preferred_element_type=jnp.float32)
    act = (jax.nn.silu(mid[:, :width]) * mid[:, width:]).astype(jnp.bfloat16)
    return jnp.dot(act, w_out, preferred_element_type=jnp.float32)


def gather_rows_by_chip(w, passenger):
    groups = lax.axis_size("group")
    ring = groups // 2
    g = lax.axis_index("group")
    y, c = g // 2, g % 2

    def shift(x, s):
        pairs = [(2 * q + k, 2 * ((q + s) % ring) + k) for q in range(ring) for k in range(2)]
        return lax.ppermute(x, "group", pairs)

    def sib(x):
        return lax.ppermute(x, "group", [(i, i ^ 1) for i in range(groups)])

    half = w.shape[0] // 2
    from_left = shift(w, 1)
    from_right = shift(w, -1)
    from_left, passenger = lax.optimization_barrier((from_left, passenger))
    far = jnp.concatenate(
        [shift(from_right[:half], -1), shift(from_left[half:], 1)], axis=0
    )
    pieces = [w, from_left, from_right, far, sib(w), sib(from_left), sib(from_right), sib(far)]
    return pieces, passenger


def chip_gather_order():
    ring = lax.axis_size("group") // 2
    g = lax.axis_index("group")
    y, c = g // 2, g % 2
    ys = (y + jnp.array([0, -1, 1, 2], jnp.int32) + ring) % ring
    return jnp.concatenate([2 * ys + c, 2 * ys + 1 - c])


def _pieces_dot_kernel(ctx_ref, *refs):
    out_ref = refs[-1]
    width = refs[0].shape[0]
    acc = None
    for i, piece in enumerate(refs[:-1]):
        term = jnp.dot(
            ctx_ref[:, i * width:(i + 1) * width], piece[...], preferred_element_type=jnp.float32
        )
        acc = term if acc is None else acc + term
    out_ref[...] = acc


def pieces_dot(ctx, pieces):
    return pl.pallas_call(
        _pieces_dot_kernel,
        out_shape=jax.ShapeDtypeStruct((ctx.shape[0], pieces[0].shape[1]), jnp.float32),
    )(ctx, *pieces)


def per_device(
    context,
    residual,
    attn_out_w,
    norm_gain,
    router_w,
    shared_in,
    shared_out,
    expert_in,
    expert_out_w,
    routes,
):
    tok_rows = residual.shape[0]
    width = residual.shape[1]
    picks = routes.shape[1]
    experts = lax.axis_size("expert")
    capacity = 4 * tok_rows * picks // (3 * experts)
    slots = experts * capacity
    flat_e = routes.reshape(-1)
    onehot = (flat_e[:, None] == jnp.arange(experts, dtype=jnp.int32)[None, :]).astype(jnp.int32)
    rank = jnp.cumsum(onehot, axis=0) - onehot
    position = jnp.sum(rank * onehot, axis=1)
    slot_of = (flat_e * capacity + position).reshape(tok_rows, picks)
    hit = slot_of[:, :, None] == jnp.arange(slots, dtype=jnp.int32)[None, None, :]
    dispatch = jnp.any(hit, axis=1).astype(jnp.bfloat16)
    block = attn_out_w.shape[0]
    groups = lax.axis_size("group")
    if groups == 8:
        src = chip_gather_order()[:, None] * block + jnp.arange(block, dtype=jnp.int32)[None, :]
        perm = (jnp.arange(context.shape[1], dtype=jnp.int32)[:, None] == src.reshape(1, -1))
        ctx_perm = jnp.dot(context, perm.astype(jnp.bfloat16), preferred_element_type=jnp.float32)
        ctx_perm = ctx_perm.astype(jnp.bfloat16).reshape(tok_rows, groups, block)
        pieces, (slot_of, dispatch, ctx_perm) = gather_rows_by_chip(
            attn_out_w, (slot_of, dispatch, ctx_perm)
        )
    else:
        pieces = [lax.all_gather(attn_out_w, "group", axis=0, tiled=True)]
        ctx_perm = context[:, None, :]
    pieces, shared_in, shared_out = lax.optimization_barrier((pieces, shared_in, shared_out))
    shared_in = lax.all_gather(shared_in, "group", axis=0, tiled=True)
    shared_out = lax.all_gather(shared_out, "group", axis=1, tiled=True)
    attn = pieces_dot(ctx_perm.reshape(tok_rows, -1), pieces)
    hidden_state = (residual.astype(jnp.float32) + attn).astype(jnp.bfloat16)
    hidden_f = hidden_state.astype(jnp.float32)
    scale = lax.rsqrt(jnp.mean(hidden_f * hidden_f, axis=-1, keepdims=True) + 1e-06)
    normed = (hidden_f * scale * norm_gain).astype(jnp.bfloat16)
    logits = jnp.dot(normed, router_w, preferred_element_type=jnp.float32)
    chosen = routes[:, :, None] == jnp.arange(experts, dtype=jnp.int32)[None, None, :]
    picked = jnp.sum(jnp.where(chosen, logits[:, None, :], 0.0), axis=-1)
    sig = jax.nn.sigmoid(picked)
    gates = sig / jnp.sum(sig, axis=1, keepdims=True)
    outgoing = jnp.dot(dispatch.T, normed, preferred_element_type=jnp.float32)
    outgoing = outgoing.astype(jnp.bfloat16).reshape(experts, capacity, width)
    hit = slot_of[:, :, None] == jnp.arange(slots, dtype=jnp.int32)[None, None, :]
    combine = jnp.sum(jnp.where(hit, gates[:, :, None], 0.0), axis=1)
    combine_hi = combine.astype(jnp.bfloat16)
    combine_lo = (combine - combine_hi.astype(jnp.float32)).astype(jnp.bfloat16)
    local_in = expert_in[0]
    local_out = expert_out_w[0]
    arrived = lax.all_to_all(outgoing, "expert", split_axis=0, concat_axis=0, tiled=True)
    flat_rows = arrived.reshape(-1, width)
    expert_rows = swiglu_rows(flat_rows, local_in, local_out).astype(jnp.bfloat16)
    expert_rows, shared_in, shared_out = lax.optimization_barrier((expert_rows, shared_in, shared_out))
    returned = lax.all_to_all(
        expert_rows.reshape(arrived.shape),
        "expert",
        split_axis=0,
        concat_axis=0,
        tiled=True,
    )
    returned = returned.reshape(slots, width)
    routed = jnp.dot(combine_hi, returned, preferred_element_type=jnp.float32)
    routed = routed + jnp.dot(combine_lo, returned, preferred_element_type=jnp.float32)
    shared_hidden = shared_out.shape[0]
    shared_mid = jnp.dot(
        normed,
        shared_in,
        preferred_element_type=jnp.float32,
    )
    shared_act = (
        jax.nn.silu(shared_mid[:, :shared_hidden]) * shared_mid[:, shared_hidden:]
    ).astype(jnp.bfloat16)
    shared_y = jnp.dot(
        shared_act,
        shared_out,
        preferred_element_type=jnp.float32,
    )
    return (hidden_f + shared_y + routed).astype(jnp.bfloat16)


def solution(mesh):
    placed = (
        P(("group", "expert"), None),
        P(("group", "expert"), None),
        P("group", None),
        P(),
        P(),
        P("group", None),
        P(None, "group"),
        P("expert", None, None),
        P("expert", None, None),
        P(("group", "expert"), None),
    )
    return jax.shard_map(
        per_device,
        mesh=mesh,
        in_specs=placed,
        out_specs=P(("group", "expert"), None),
        check_vma=False,
    )
```

```python
import jax
import jax.numpy as jnp
from jax import lax
from jax.sharding import PartitionSpec as P
from jax.experimental import pallas as pl


def swiglu_rows(rows, w_in, w_out):
    width = w_out.shape[0]
    mid = jnp.dot(rows, w_in, preferred_element_type=jnp.float32)
    act = (jax.nn.silu(mid[:, :width]) * mid[:, width:]).astype(jnp.bfloat16)
    return jnp.dot(act, w_out, preferred_element_type=jnp.float32)


def gather_rows_by_chip(w, passenger):
    groups = lax.axis_size("group")
    ring = groups // 2
    g = lax.axis_index("group")
    y, c = g // 2, g % 2

    def shift(x, s):
        pairs = [(2 * q + k, 2 * ((q + s) % ring) + k) for q in range(ring) for k in range(2)]
        return lax.ppermute(x, "group", pairs)

    def sib(x):
        return lax.ppermute(x, "group", [(i, i ^ 1) for i in range(groups)])

    half = w.shape[0] // 2
    from_left = shift(w, 1)
    from_right = shift(w, -1)
    from_left, passenger = lax.optimization_barrier((from_left, passenger))
    far = jnp.concatenate(
        [shift(from_right[:half], -1), shift(from_left[half:], 1)], axis=0
    )
    pieces = [w, from_left, from_right, far, sib(w), sib(from_left), sib(from_right), sib(far)]
    return pieces, passenger


def chip_gather_order():
    ring = lax.axis_size("group") // 2
    g = lax.axis_index("group")
    y, c = g // 2, g % 2
    ys = (y + jnp.array([0, -1, 1, 2], jnp.int32) + ring) % ring
    return jnp.concatenate([2 * ys + c, 2 * ys + 1 - c])


def _pieces_dot_kernel(ctx_ref, *refs):
    out_ref = refs[-1]
    width = refs[0].shape[0]
    acc = None
    for i, piece in enumerate(refs[:-1]):
        term = jnp.dot(
            ctx_ref[:, i * width:(i + 1) * width], piece[...], preferred_element_type=jnp.float32
        )
        acc = term if acc is None else acc + term
    out_ref[...] = acc


def pieces_dot(ctx, pieces):
    return pl.pallas_call(
        _pieces_dot_kernel,
        out_shape=jax.ShapeDtypeStruct((ctx.shape[0], pieces[0].shape[1]), jnp.float32),
    )(ctx, *pieces)


def per_device(
    context,
    residual,
    attn_out_w,
    norm_gain,
    router_w,
    shared_in,
    shared_out,
    expert_in,
    expert_out_w,
    routes,
):
    tok_rows = residual.shape[0]
    width = residual.shape[1]
    picks = routes.shape[1]
    experts = lax.axis_size("expert")
    capacity = 4 * tok_rows * picks // (3 * experts)
    slots = experts * capacity
    flat_e = routes.reshape(-1)
    onehot = (flat_e[:, None] == jnp.arange(experts, dtype=jnp.int32)[None, :]).astype(jnp.int32)
    rank = jnp.cumsum(onehot, axis=0) - onehot
    position = jnp.sum(rank * onehot, axis=1)
    slot_of = (flat_e * capacity + position).reshape(tok_rows, picks)
    hit = slot_of[:, :, None] == jnp.arange(slots, dtype=jnp.int32)[None, None, :]
    dispatch = jnp.any(hit, axis=1).astype(jnp.bfloat16)
    block = attn_out_w.shape[0]
    groups = lax.axis_size("group")
    if groups == 8:
        src = chip_gather_order()[:, None] * block + jnp.arange(block, dtype=jnp.int32)[None, :]
        perm = (jnp.arange(context.shape[1], dtype=jnp.int32)[:, None] == src.reshape(1, -1))
        ctx_perm = jnp.dot(context, perm.astype(jnp.bfloat16), preferred_element_type=jnp.float32)
        ctx_perm = ctx_perm.astype(jnp.bfloat16).reshape(tok_rows, groups, block)
        pieces, (slot_of, dispatch, ctx_perm) = gather_rows_by_chip(
            attn_out_w, (slot_of, dispatch, ctx_perm)
        )
    else:
        pieces = [lax.all_gather(attn_out_w, "group", axis=0, tiled=True)]
        ctx_perm = context[:, None, :]
    pieces, shared_in, shared_out = lax.optimization_barrier((pieces, shared_in, shared_out))
    shared_in = lax.all_gather(shared_in, "group", axis=0, tiled=True)
    shared_out = lax.all_gather(shared_out, "group", axis=1, tiled=True)
    attn = pieces_dot(ctx_perm.reshape(tok_rows, -1), pieces)
    hidden_state = (residual.astype(jnp.float32) + attn).astype(jnp.bfloat16)
    hidden_f = hidden_state.astype(jnp.float32)
    scale = lax.rsqrt(jnp.mean(hidden_f * hidden_f, axis=-1, keepdims=True) + 1e-06)
    normed = (hidden_f * scale * norm_gain).astype(jnp.bfloat16)
    logits = jnp.dot(normed, router_w, preferred_element_type=jnp.float32)
    chosen = routes[:, :, None] == jnp.arange(experts, dtype=jnp.int32)[None, None, :]
    picked = jnp.sum(jnp.where(chosen, logits[:, None, :], 0.0), axis=-1)
    sig = jax.nn.sigmoid(picked)
    gates = sig / jnp.sum(sig, axis=1, keepdims=True)
    outgoing = jnp.dot(dispatch.T, normed, preferred_element_type=jnp.float32)
    outgoing = outgoing.astype(jnp.bfloat16).reshape(experts, capacity, width)
    hit = slot_of[:, :, None] == jnp.arange(slots, dtype=jnp.int32)[None, None, :]
    combine = jnp.sum(jnp.where(hit, gates[:, :, None], 0.0), axis=1)
    combine_hi = combine.astype(jnp.bfloat16)
    combine_lo = (combine - combine_hi.astype(jnp.float32)).astype(jnp.bfloat16)
    local_in = expert_in[0]
    local_out = expert_out_w[0]
    arrived = lax.all_to_all(outgoing, "expert", split_axis=0, concat_axis=0, tiled=True)
    flat_rows = arrived.reshape(-1, width)
    expert_rows = swiglu_rows(flat_rows, local_in, local_out).astype(jnp.bfloat16)
    expert_rows, shared_in, shared_out = lax.optimization_barrier((expert_rows, shared_in, shared_out))
    returned = lax.all_to_all(
        expert_rows.reshape(arrived.shape),
        "expert",
        split_axis=0,
        concat_axis=0,
        tiled=True,
    )
    returned = returned.reshape(slots, width)
    both = jnp.dot(
        jnp.concatenate([combine_hi, combine_lo], axis=0), returned, preferred_element_type=jnp.float32
    )
    routed = both[:tok_rows] + both[tok_rows:]
    shared_hidden = shared_out.shape[0]
    shared_mid = jnp.dot(
        normed,
        shared_in,
        preferred_element_type=jnp.float32,
    )
    shared_act = (
        jax.nn.silu(shared_mid[:, :shared_hidden]) * shared_mid[:, shared_hidden:]
    ).astype(jnp.bfloat16)
    shared_y = jnp.dot(
        shared_act,
        shared_out,
        preferred_element_type=jnp.float32,
    )
    return (hidden_f + shared_y + routed).astype(jnp.bfloat16)


def solution(mesh):
    placed = (
        P(("group", "expert"), None),
        P(("group", "expert"), None),
        P("group", None),
        P(),
        P(),
        P("group", None),
        P(None, "group"),
        P("expert", None, None),
        P("expert", None, None),
        P(("group", "expert"), None),
    )
    return jax.shard_map(
        per_device,
        mesh=mesh,
        in_specs=placed,
        out_specs=P(("group", "expert"), None),
        check_vma=False,
    )
```

```python
import jax
import jax.numpy as jnp
from jax import lax
from jax.sharding import PartitionSpec as P
from jax.experimental import pallas as pl


def swiglu_rows(rows, w_in, w_out):
    width = w_out.shape[0]
    mid = jnp.dot(rows, w_in, preferred_element_type=jnp.float32)
    act = (jax.nn.silu(mid[:, :width]) * mid[:, width:]).astype(jnp.bfloat16)
    return jnp.dot(act, w_out, preferred_element_type=jnp.float32)


def gather_rows_by_chip(w, passenger):
    groups = lax.axis_size("group")
    ring = groups // 2
    g = lax.axis_index("group")
    y, c = g // 2, g % 2

    def shift(x, s):
        pairs = [(2 * q + k, 2 * ((q + s) % ring) + k) for q in range(ring) for k in range(2)]
        return lax.ppermute(x, "group", pairs)

    def sib(x):
        return lax.ppermute(x, "group", [(i, i ^ 1) for i in range(groups)])

    half = w.shape[0] // 2
    from_left = shift(w, 1)
    from_right = shift(w, -1)
    from_left, passenger = lax.optimization_barrier((from_left, passenger))
    far = jnp.concatenate(
        [shift(from_right[:half], -1), shift(from_left[half:], 1)], axis=0
    )
    pieces = [w, from_left, from_right, far, sib(w), sib(from_left), sib(from_right), sib(far)]
    return pieces, passenger


def chip_gather_order():
    ring = lax.axis_size("group") // 2
    g = lax.axis_index("group")
    y, c = g // 2, g % 2
    ys = (y + jnp.array([0, -1, 1, 2], jnp.int32) + ring) % ring
    return jnp.concatenate([2 * ys + c, 2 * ys + 1 - c])


def _pieces_dot_kernel(ctx_ref, *refs):
    out_ref = refs[-1]
    width = refs[0].shape[0]
    acc = None
    for i, piece in enumerate(refs[:-1]):
        term = jnp.dot(
            ctx_ref[:, i * width:(i + 1) * width], piece[...], preferred_element_type=jnp.float32
        )
        acc = term if acc is None else acc + term
    out_ref[...] = acc


def pieces_dot(ctx, pieces):
    return pl.pallas_call(
        _pieces_dot_kernel,
        out_shape=jax.ShapeDtypeStruct((ctx.shape[0], pieces[0].shape[1]), jnp.float32),
    )(ctx, *pieces)


def per_device(
    context,
    residual,
    attn_out_w,
    norm_gain,
    router_w,
    shared_in,
    shared_out,
    expert_in,
    expert_out_w,
    routes,
):
    tok_rows = residual.shape[0]
    width = residual.shape[1]
    picks = routes.shape[1]
    experts = lax.axis_size("expert")
    capacity = 4 * tok_rows * picks // (3 * experts)
    slots = experts * capacity
    flat_e = routes.reshape(-1)
    onehot = (flat_e[:, None] == jnp.arange(experts, dtype=jnp.int32)[None, :]).astype(jnp.int32)
    rank = jnp.cumsum(onehot, axis=0) - onehot
    position = jnp.sum(rank * onehot, axis=1)
    slot_of = (flat_e * capacity + position).reshape(tok_rows, picks)
    hit = slot_of[:, :, None] == jnp.arange(slots, dtype=jnp.int32)[None, None, :]
    dispatch = jnp.any(hit, axis=1).astype(jnp.bfloat16)
    block = attn_out_w.shape[0]
    groups = lax.axis_size("group")
    if groups == 8:
        src = chip_gather_order()[:, None] * block + jnp.arange(block, dtype=jnp.int32)[None, :]
        perm = (jnp.arange(context.shape[1], dtype=jnp.int32)[:, None] == src.reshape(1, -1))
        ctx_perm = jnp.dot(context, perm.astype(jnp.bfloat16), preferred_element_type=jnp.float32)
        ctx_perm = ctx_perm.astype(jnp.bfloat16).reshape(tok_rows, groups, block)
        pieces, (slot_of, dispatch, ctx_perm) = gather_rows_by_chip(
            attn_out_w, (slot_of, dispatch, ctx_perm)
        )
    else:
        pieces = [lax.all_gather(attn_out_w, "group", axis=0, tiled=True)]
        ctx_perm = context[:, None, :]
    pieces, shared_in, shared_out = lax.optimization_barrier((pieces, shared_in, shared_out))
    shared_in = lax.all_gather(shared_in, "group", axis=0, tiled=True)
    shared_out = lax.all_gather(shared_out, "group", axis=1, tiled=True)
    attn = pieces_dot(ctx_perm.reshape(tok_rows, -1), pieces)
    hidden_state = (residual.astype(jnp.float32) + attn).astype(jnp.bfloat16)
    hidden_f = hidden_state.astype(jnp.float32)
    scale = lax.rsqrt(jnp.mean(hidden_f * hidden_f, axis=-1, keepdims=True) + 1e-06)
    normed = (hidden_f * scale * norm_gain).astype(jnp.bfloat16)
    logits = jnp.dot(normed, router_w, preferred_element_type=jnp.float32)
    chosen = routes[:, :, None] == jnp.arange(experts, dtype=jnp.int32)[None, None, :]
    picked = jnp.sum(jnp.where(chosen, logits[:, None, :], 0.0), axis=-1)
    sig = jax.nn.sigmoid(picked)
    gates = sig / jnp.sum(sig, axis=1, keepdims=True)
    outgoing = jnp.dot(dispatch.T, normed, preferred_element_type=jnp.float32)
    outgoing = outgoing.astype(jnp.bfloat16).reshape(experts, capacity, width)
    hit = slot_of[:, :, None] == jnp.arange(slots, dtype=jnp.int32)[None, None, :]
    combine = jnp.sum(jnp.where(hit, gates[:, :, None], 0.0), axis=1)
    combine_hi = combine.astype(jnp.bfloat16)
    combine_lo = (combine - combine_hi.astype(jnp.float32)).astype(jnp.bfloat16)
    local_in = expert_in[0]
    local_out = expert_out_w[0]
    arrived = lax.all_to_all(outgoing, "expert", split_axis=0, concat_axis=0, tiled=True)
    flat_rows = arrived.reshape(-1, width)
    expert_rows = swiglu_rows(flat_rows, local_in, local_out).astype(jnp.bfloat16)
    expert_rows, shared_in, shared_out = lax.optimization_barrier((expert_rows, shared_in, shared_out))
    returned = lax.all_to_all(
        expert_rows.reshape(arrived.shape),
        "expert",
        split_axis=0,
        concat_axis=0,
        tiled=True,
    )
    returned = returned.reshape(slots, width)
    both = jnp.dot(
        jnp.concatenate([combine_hi, combine_lo], axis=0), returned, preferred_element_type=jnp.float32
    )
    routed = both[:tok_rows] + both[tok_rows:]
    shared_hidden = shared_out.shape[0]
    shared_mid = jnp.dot(
        normed,
        shared_in,
        preferred_element_type=jnp.float32,
    )
    shared_act = (
        jax.nn.silu(shared_mid[:, :shared_hidden]) * shared_mid[:, shared_hidden:]
    ).astype(jnp.bfloat16)
    shared_y = jnp.dot(
        shared_act,
        shared_out,
        preferred_element_type=jnp.float32,
    )
    shared_y = lax.optimization_barrier(shared_y)
    return (hidden_f + shared_y + routed).astype(jnp.bfloat16)


def solution(mesh):
    placed = (
        P(("group", "expert"), None),
        P(("group", "expert"), None),
        P("group", None),
        P(),
        P(),
        P("group", None),
        P(None, "group"),
        P("expert", None, None),
        P("expert", None, None),
        P(("group", "expert"), None),
    )
    return jax.shard_map(
        per_device,
        mesh=mesh,
        in_specs=placed,
        out_specs=P(("group", "expert"), None),
        check_vma=False,
    )
```

```python
import jax
import jax.numpy as jnp
from jax import lax
from jax.sharding import PartitionSpec as P
from jax.experimental import pallas as pl


def swiglu_rows(rows, w_in, w_out):
    width = w_out.shape[0]
    mid = jnp.dot(rows, w_in, preferred_element_type=jnp.float32)
    act = (jax.nn.silu(mid[:, :width]) * mid[:, width:]).astype(jnp.bfloat16)
    return jnp.dot(act, w_out, preferred_element_type=jnp.float32)


def gather_rows_by_chip(w, passenger):
    groups = lax.axis_size("group")
    ring = groups // 2
    g = lax.axis_index("group")
    y, c = g // 2, g % 2

    def shift(x, s):
        pairs = [(2 * q + k, 2 * ((q + s) % ring) + k) for q in range(ring) for k in range(2)]
        return lax.ppermute(x, "group", pairs)

    def sib(x):
        return lax.ppermute(x, "group", [(i, i ^ 1) for i in range(groups)])

    half = w.shape[0] // 2
    from_left = shift(w, 1)
    from_right = shift(w, -1)
    from_left, passenger = lax.optimization_barrier((from_left, passenger))
    far = jnp.concatenate(
        [shift(from_right[:half], -1), shift(from_left[half:], 1)], axis=0
    )
    pieces = [w, from_left, from_right, far, sib(w), sib(from_left), sib(from_right), sib(far)]
    return pieces, passenger


def chip_gather_order():
    ring = lax.axis_size("group") // 2
    g = lax.axis_index("group")
    y, c = g // 2, g % 2
    ys = (y + jnp.array([0, -1, 1, 2], jnp.int32) + ring) % ring
    return jnp.concatenate([2 * ys + c, 2 * ys + 1 - c])


def _pieces_dot_kernel(ctx_ref, *refs):
    out_ref = refs[-1]
    width = refs[0].shape[0]
    acc = None
    for i, piece in enumerate(refs[:-1]):
        term = jnp.dot(
            ctx_ref[:, i * width:(i + 1) * width], piece[...], preferred_element_type=jnp.float32
        )
        acc = term if acc is None else acc + term
    out_ref[...] = acc


def pieces_dot(ctx, pieces):
    return pl.pallas_call(
        _pieces_dot_kernel,
        out_shape=jax.ShapeDtypeStruct((ctx.shape[0], pieces[0].shape[1]), jnp.float32),
    )(ctx, *pieces)


def per_device(
    context,
    residual,
    attn_out_w,
    norm_gain,
    router_w,
    shared_in,
    shared_out,
    expert_in,
    expert_out_w,
    routes,
):
    tok_rows = residual.shape[0]
    width = residual.shape[1]
    picks = routes.shape[1]
    experts = lax.axis_size("expert")
    capacity = 4 * tok_rows * picks // (3 * experts)
    slots = experts * capacity
    flat_e = routes.reshape(-1)
    onehot = (flat_e[:, None] == jnp.arange(experts, dtype=jnp.int32)[None, :]).astype(jnp.int32)
    rank = jnp.cumsum(onehot, axis=0) - onehot
    position = jnp.sum(rank * onehot, axis=1)
    slot_of = (flat_e * capacity + position).reshape(tok_rows, picks)
    hit = slot_of[:, :, None] == jnp.arange(slots, dtype=jnp.int32)[None, None, :]
    dispatch = jnp.any(hit, axis=1).astype(jnp.bfloat16)
    block = attn_out_w.shape[0]
    groups = lax.axis_size("group")
    if groups == 8:
        src = chip_gather_order()[:, None] * block + jnp.arange(block, dtype=jnp.int32)[None, :]
        perm = (jnp.arange(context.shape[1], dtype=jnp.int32)[:, None] == src.reshape(1, -1))
        ctx_perm = jnp.dot(context, perm.astype(jnp.bfloat16), preferred_element_type=jnp.float32)
        ctx_perm = ctx_perm.astype(jnp.bfloat16)
        pieces, (slot_of, dispatch, ctx_perm) = gather_rows_by_chip(
            attn_out_w, (slot_of, dispatch, ctx_perm)
        )
    else:
        pieces = [lax.all_gather(attn_out_w, "group", axis=0, tiled=True)]
        ctx_perm = context
    pieces, shared_in, shared_out = lax.optimization_barrier((pieces, shared_in, shared_out))
    shared_in = lax.all_gather(shared_in, "group", axis=0, tiled=True)
    shared_out = lax.all_gather(shared_out, "group", axis=1, tiled=True)
    attn = pieces_dot(ctx_perm, pieces)
    hidden_state = (residual.astype(jnp.float32) + attn).astype(jnp.bfloat16)
    hidden_f = hidden_state.astype(jnp.float32)
    scale = lax.rsqrt(jnp.mean(hidden_f * hidden_f, axis=-1, keepdims=True) + 1e-06)
    normed = (hidden_f * scale * norm_gain).astype(jnp.bfloat16)
    logits = jnp.dot(normed, router_w, preferred_element_type=jnp.float32)
    chosen = routes[:, :, None] == jnp.arange(experts, dtype=jnp.int32)[None, None, :]
    picked = jnp.sum(jnp.where(chosen, logits[:, None, :], 0.0), axis=-1)
    sig = jax.nn.sigmoid(picked)
    gates = sig / jnp.sum(sig, axis=1, keepdims=True)
    outgoing = jnp.dot(dispatch.T, normed, preferred_element_type=jnp.float32)
    outgoing = outgoing.astype(jnp.bfloat16).reshape(experts, capacity, width)
    hit = slot_of[:, :, None] == jnp.arange(slots, dtype=jnp.int32)[None, None, :]
    combine = jnp.sum(jnp.where(hit, gates[:, :, None], 0.0), axis=1)
    combine_hi = combine.astype(jnp.bfloat16)
    combine_lo = (combine - combine_hi.astype(jnp.float32)).astype(jnp.bfloat16)
    local_in = expert_in[0]
    local_out = expert_out_w[0]
    arrived = lax.all_to_all(outgoing, "expert", split_axis=0, concat_axis=0, tiled=True)
    flat_rows = arrived.reshape(-1, width)
    expert_rows = swiglu_rows(flat_rows, local_in, local_out).astype(jnp.bfloat16)
    expert_rows, shared_in, shared_out = lax.optimization_barrier((expert_rows, shared_in, shared_out))
    returned = lax.all_to_all(
        expert_rows.reshape(arrived.shape),
        "expert",
        split_axis=0,
        concat_axis=0,
        tiled=True,
    )
    returned = returned.reshape(slots, width)
    both = jnp.dot(
        jnp.concatenate([combine_hi, combine_lo], axis=0), returned, preferred_element_type=jnp.float32
    )
    routed = both[:tok_rows] + both[tok_rows:]
    shared_hidden = shared_out.shape[0]
    shared_mid = jnp.dot(
        normed,
        shared_in,
        preferred_element_type=jnp.float32,
    )
    shared_act = (
        jax.nn.silu(shared_mid[:, :shared_hidden]) * shared_mid[:, shared_hidden:]
    ).astype(jnp.bfloat16)
    shared_y = jnp.dot(
        shared_act,
        shared_out,
        preferred_element_type=jnp.float32,
    )
    shared_y = lax.optimization_barrier(shared_y)
    return (hidden_f + shared_y + routed).astype(jnp.bfloat16)


def solution(mesh):
    placed = (
        P(("group", "expert"), None),
        P(("group", "expert"), None),
        P("group", None),
        P(),
        P(),
        P("group", None),
        P(None, "group"),
        P("expert", None, None),
        P("expert", None, None),
        P(("group", "expert"), None),
    )
    return jax.shard_map(
        per_device,
        mesh=mesh,
        in_specs=placed,
        out_specs=P(("group", "expert"), None),
        check_vma=False,
    )
```

```python
import jax
import jax.numpy as jnp
from jax import lax
from jax.sharding import PartitionSpec as P
from jax.experimental import pallas as pl


def swiglu_rows(rows, w_in, w_out):
    width = w_out.shape[0]
    mid = jnp.dot(rows, w_in, preferred_element_type=jnp.float32)
    act = (jax.nn.silu(mid[:, :width]) * mid[:, width:]).astype(jnp.bfloat16)
    return jnp.dot(act, w_out, preferred_element_type=jnp.float32)


def gather_rows_by_chip(w, passenger):
    groups = lax.axis_size("group")
    ring = groups // 2
    g = lax.axis_index("group")
    y, c = g // 2, g % 2

    def shift(x, s):
        pairs = [(2 * q + k, 2 * ((q + s) % ring) + k) for q in range(ring) for k in range(2)]
        return lax.ppermute(x, "group", pairs)

    def sib(x):
        return lax.ppermute(x, "group", [(i, i ^ 1) for i in range(groups)])

    half = w.shape[0] // 2
    from_left = shift(w, 1)
    from_right = shift(w, -1)
    from_left, passenger = lax.optimization_barrier((from_left, passenger))
    far = jnp.concatenate(
        [shift(from_right[:half], -1), shift(from_left[half:], 1)], axis=0
    )
    pieces = [w, from_left, from_right, far, sib(w), sib(from_left), sib(from_right), sib(far)]
    return pieces, passenger


def chip_gather_order():
    ring = lax.axis_size("group") // 2
    g = lax.axis_index("group")
    y, c = g // 2, g % 2
    ys = (y + jnp.array([0, -1, 1, 2], jnp.int32) + ring) % ring
    return jnp.concatenate([2 * ys + c, 2 * ys + 1 - c])


def _pieces_dot_kernel(ctx_ref, *refs):
    out_ref = refs[-1]
    width = refs[0].shape[0]
    acc = None
    for i, piece in enumerate(refs[:-1]):
        term = jnp.dot(
            ctx_ref[:, i * width:(i + 1) * width], piece[...], preferred_element_type=jnp.float32
        )
        acc = term if acc is None else acc + term
    out_ref[...] = acc


def pieces_dot(ctx, pieces):
    return pl.pallas_call(
        _pieces_dot_kernel,
        out_shape=jax.ShapeDtypeStruct((ctx.shape[0], pieces[0].shape[1]), jnp.float32),
    )(ctx, *pieces)


def _combine_kernel(comb_ref, ret_ref, hid_ref, sh_ref, out_ref):
    rows = hid_ref.shape[0]
    both = jnp.dot(comb_ref[...], ret_ref[...], preferred_element_type=jnp.float32)
    routed = both[:rows] + both[rows:]
    out_ref[...] = (hid_ref[...] + sh_ref[...] + routed).astype(out_ref.dtype)


def combine_rows(comb, returned, hidden_f, shared_y, cols=512):
    rows, width = hidden_f.shape
    slots = returned.shape[0]
    cols = min(cols, width)
    return pl.pallas_call(
        _combine_kernel,
        out_shape=jax.ShapeDtypeStruct((rows, width), jnp.bfloat16),
        grid=(width // cols,),
        in_specs=[
            pl.BlockSpec((2 * rows, slots), lambda j: (0, 0)),
            pl.BlockSpec((slots, cols), lambda j: (0, j)),
            pl.BlockSpec((rows, cols), lambda j: (0, j)),
            pl.BlockSpec((rows, cols), lambda j: (0, j)),
        ],
        out_specs=pl.BlockSpec((rows, cols), lambda j: (0, j)),
    )(comb, returned, hidden_f, shared_y)


def per_device(
    context,
    residual,
    attn_out_w,
    norm_gain,
    router_w,
    shared_in,
    shared_out,
    expert_in,
    expert_out_w,
    routes,
):
    tok_rows = residual.shape[0]
    width = residual.shape[1]
    picks = routes.shape[1]
    experts = lax.axis_size("expert")
    capacity = 4 * tok_rows * picks // (3 * experts)
    slots = experts * capacity
    flat_e = routes.reshape(-1)
    onehot = (flat_e[:, None] == jnp.arange(experts, dtype=jnp.int32)[None, :]).astype(jnp.int32)
    rank = jnp.cumsum(onehot, axis=0) - onehot
    position = jnp.sum(rank * onehot, axis=1)
    slot_of = (flat_e * capacity + position).reshape(tok_rows, picks)
    hit = slot_of[:, :, None] == jnp.arange(slots, dtype=jnp.int32)[None, None, :]
    dispatch = jnp.any(hit, axis=1).astype(jnp.bfloat16)
    block = attn_out_w.shape[0]
    groups = lax.axis_size("group")
    if groups == 8:
        src = chip_gather_order()[:, None] * block + jnp.arange(block, dtype=jnp.int32)[None, :]
        perm = (jnp.arange(context.shape[1], dtype=jnp.int32)[:, None] == src.reshape(1, -1))
        ctx_perm = jnp.dot(context, perm.astype(jnp.bfloat16), preferred_element_type=jnp.float32)
        ctx_perm = ctx_perm.astype(jnp.bfloat16)
        pieces, (slot_of, dispatch, ctx_perm) = gather_rows_by_chip(
            attn_out_w, (slot_of, dispatch, ctx_perm)
        )
    else:
        pieces = [lax.all_gather(attn_out_w, "group", axis=0, tiled=True)]
        ctx_perm = context
    pieces, shared_in, shared_out = lax.optimization_barrier((pieces, shared_in, shared_out))
    shared_in = lax.all_gather(shared_in, "group", axis=0, tiled=True)
    shared_out = lax.all_gather(shared_out, "group", axis=1, tiled=True)
    attn = pieces_dot(ctx_perm, pieces)
    hidden_state = (residual.astype(jnp.float32) + attn).astype(jnp.bfloat16)
    hidden_f = hidden_state.astype(jnp.float32)
    scale = lax.rsqrt(jnp.mean(hidden_f * hidden_f, axis=-1, keepdims=True) + 1e-06)
    normed = (hidden_f * scale * norm_gain).astype(jnp.bfloat16)
    logits = jnp.dot(normed, router_w, preferred_element_type=jnp.float32)
    chosen = routes[:, :, None] == jnp.arange(experts, dtype=jnp.int32)[None, None, :]
    picked = jnp.sum(jnp.where(chosen, logits[:, None, :], 0.0), axis=-1)
    sig = jax.nn.sigmoid(picked)
    gates = sig / jnp.sum(sig, axis=1, keepdims=True)
    outgoing = jnp.dot(dispatch.T, normed, preferred_element_type=jnp.float32)
    outgoing = outgoing.astype(jnp.bfloat16).reshape(experts, capacity, width)
    hit = slot_of[:, :, None] == jnp.arange(slots, dtype=jnp.int32)[None, None, :]
    combine = jnp.sum(jnp.where(hit, gates[:, :, None], 0.0), axis=1)
    combine_hi = combine.astype(jnp.bfloat16)
    combine_lo = (combine - combine_hi.astype(jnp.float32)).astype(jnp.bfloat16)
    local_in = expert_in[0]
    local_out = expert_out_w[0]
    arrived = lax.all_to_all(outgoing, "expert", split_axis=0, concat_axis=0, tiled=True)
    flat_rows = arrived.reshape(-1, width)
    expert_rows = swiglu_rows(flat_rows, local_in, local_out).astype(jnp.bfloat16)
    expert_rows, shared_in, shared_out = lax.optimization_barrier((expert_rows, shared_in, shared_out))
    returned = lax.all_to_all(
        expert_rows.reshape(arrived.shape),
        "expert",
        split_axis=0,
        concat_axis=0,
        tiled=True,
    )
    returned = returned.reshape(slots, width)
    shared_hidden = shared_out.shape[0]
    shared_mid = jnp.dot(
        normed,
        shared_in,
        preferred_element_type=jnp.float32,
    )
    shared_act = (
        jax.nn.silu(shared_mid[:, :shared_hidden]) * shared_mid[:, shared_hidden:]
    ).astype(jnp.bfloat16)
    shared_y = jnp.dot(
        shared_act,
        shared_out,
        preferred_element_type=jnp.float32,
    )
    shared_y = lax.optimization_barrier(shared_y)
    return combine_rows(jnp.concatenate([combine_hi, combine_lo], axis=0), returned, hidden_f, shared_y)


def solution(mesh):
    placed = (
        P(("group", "expert"), None),
        P(("group", "expert"), None),
        P("group", None),
        P(),
        P(),
        P("group", None),
        P(None, "group"),
        P("expert", None, None),
        P("expert", None, None),
        P(("group", "expert"), None),
    )
    return jax.shard_map(
        per_device,
        mesh=mesh,
        in_specs=placed,
        out_specs=P(("group", "expert"), None),
        check_vma=False,
    )
```

```python
import jax
import jax.numpy as jnp
from jax import lax
from jax.sharding import PartitionSpec as P
from jax.experimental import pallas as pl


def swiglu_rows(rows, w_in, w_out):
    width = w_out.shape[0]
    mid = jnp.dot(rows, w_in, preferred_element_type=jnp.float32)
    act = (jax.nn.silu(mid[:, :width]) * mid[:, width:]).astype(jnp.bfloat16)
    return jnp.dot(act, w_out, preferred_element_type=jnp.float32)


def gather_rows_by_chip(w, passenger):
    groups = lax.axis_size("group")
    ring = groups // 2
    g = lax.axis_index("group")
    y, c = g // 2, g % 2

    def shift(x, s):
        pairs = [(2 * q + k, 2 * ((q + s) % ring) + k) for q in range(ring) for k in range(2)]
        return lax.ppermute(x, "group", pairs)

    def sib(x):
        return lax.ppermute(x, "group", [(i, i ^ 1) for i in range(groups)])

    half = w.shape[0] // 2
    from_left = shift(w, 1)
    from_right = shift(w, -1)
    from_left, passenger = lax.optimization_barrier((from_left, passenger))
    far = jnp.concatenate(
        [shift(from_right[:half], -1), shift(from_left[half:], 1)], axis=0
    )
    pieces = [w, from_left, from_right, far, sib(w), sib(from_left), sib(from_right), sib(far)]
    return pieces, passenger


def chip_gather_order():
    ring = lax.axis_size("group") // 2
    g = lax.axis_index("group")
    y, c = g // 2, g % 2
    ys = (y + jnp.array([0, -1, 1, 2], jnp.int32) + ring) % ring
    return jnp.concatenate([2 * ys + c, 2 * ys + 1 - c])


def _attn_norm_kernel(ctx_ref, res_ref, gain_ref, *refs):
    hid_ref, normed_ref = refs[-2:]
    pieces = refs[:-2]
    width = pieces[0].shape[0]
    acc = None
    for i, piece in enumerate(pieces):
        term = jnp.dot(
            ctx_ref[:, i * width:(i + 1) * width], piece[...], preferred_element_type=jnp.float32
        )
        acc = term if acc is None else acc + term
    hidden = (res_ref[...].astype(jnp.float32) + acc).astype(jnp.bfloat16).astype(jnp.float32)
    scale = lax.rsqrt(jnp.mean(hidden * hidden, axis=-1, keepdims=True) + 1e-06)
    hid_ref[...] = hidden
    normed_ref[...] = (hidden * scale * gain_ref[...]).astype(jnp.bfloat16)


def attn_norm(ctx, pieces, residual, norm_gain):
    shape = (ctx.shape[0], pieces[0].shape[1])
    return pl.pallas_call(
        _attn_norm_kernel,
        out_shape=(
            jax.ShapeDtypeStruct(shape, jnp.float32),
            jax.ShapeDtypeStruct(shape, jnp.bfloat16),
        ),
    )(ctx, residual, norm_gain.reshape(1, -1), *pieces)


def per_device(
    context,
    residual,
    attn_out_w,
    norm_gain,
    router_w,
    shared_in,
    shared_out,
    expert_in,
    expert_out_w,
    routes,
):
    tok_rows = residual.shape[0]
    width = residual.shape[1]
    picks = routes.shape[1]
    experts = lax.axis_size("expert")
    capacity = 4 * tok_rows * picks // (3 * experts)
    slots = experts * capacity
    flat_e = routes.reshape(-1)
    onehot = (flat_e[:, None] == jnp.arange(experts, dtype=jnp.int32)[None, :]).astype(jnp.int32)
    rank = jnp.cumsum(onehot, axis=0) - onehot
    position = jnp.sum(rank * onehot, axis=1)
    slot_of = (flat_e * capacity + position).reshape(tok_rows, picks)
    hit = slot_of[:, :, None] == jnp.arange(slots, dtype=jnp.int32)[None, None, :]
    dispatch = jnp.any(hit, axis=1).astype(jnp.bfloat16)
    block = attn_out_w.shape[0]
    groups = lax.axis_size("group")
    if groups == 8:
        src = chip_gather_order()[:, None] * block + jnp.arange(block, dtype=jnp.int32)[None, :]
        perm = (jnp.arange(context.shape[1], dtype=jnp.int32)[:, None] == src.reshape(1, -1))
        ctx_perm = jnp.dot(context, perm.astype(jnp.bfloat16), preferred_element_type=jnp.float32)
        ctx_perm = ctx_perm.astype(jnp.bfloat16)
        pieces, (slot_of, dispatch, ctx_perm) = gather_rows_by_chip(
            attn_out_w, (slot_of, dispatch, ctx_perm)
        )
    else:
        pieces = [lax.all_gather(attn_out_w, "group", axis=0, tiled=True)]
        ctx_perm = context
    pieces, shared_in, shared_out = lax.optimization_barrier((pieces, shared_in, shared_out))
    shared_in = lax.all_gather(shared_in, "group", axis=0, tiled=True)
    shared_out = lax.all_gather(shared_out, "group", axis=1, tiled=True)
    hidden_f, normed = attn_norm(ctx_perm, pieces, residual, norm_gain)
    logits = jnp.dot(normed, router_w, preferred_element_type=jnp.float32)
    chosen = routes[:, :, None] == jnp.arange(experts, dtype=jnp.int32)[None, None, :]
    picked = jnp.sum(jnp.where(chosen, logits[:, None, :], 0.0), axis=-1)
    sig = jax.nn.sigmoid(picked)
    gates = sig / jnp.sum(sig, axis=1, keepdims=True)
    outgoing = jnp.dot(dispatch.T, normed, preferred_element_type=jnp.float32)
    outgoing = outgoing.astype(jnp.bfloat16).reshape(experts, capacity, width)
    hit = slot_of[:, :, None] == jnp.arange(slots, dtype=jnp.int32)[None, None, :]
    combine = jnp.sum(jnp.where(hit, gates[:, :, None], 0.0), axis=1)
    combine_hi = combine.astype(jnp.bfloat16)
    combine_lo = (combine - combine_hi.astype(jnp.float32)).astype(jnp.bfloat16)
    local_in = expert_in[0]
    local_out = expert_out_w[0]
    arrived = lax.all_to_all(outgoing, "expert", split_axis=0, concat_axis=0, tiled=True)
    flat_rows = arrived.reshape(-1, width)
    expert_rows = swiglu_rows(flat_rows, local_in, local_out).astype(jnp.bfloat16)
    expert_rows, shared_in, shared_out = lax.optimization_barrier((expert_rows, shared_in, shared_out))
    returned = lax.all_to_all(
        expert_rows.reshape(arrived.shape),
        "expert",
        split_axis=0,
        concat_axis=0,
        tiled=True,
    )
    returned = returned.reshape(slots, width)
    both = jnp.dot(
        jnp.concatenate([combine_hi, combine_lo], axis=0), returned, preferred_element_type=jnp.float32
    )
    routed = both[:tok_rows] + both[tok_rows:]
    shared_hidden = shared_out.shape[0]
    shared_mid = jnp.dot(
        normed,
        shared_in,
        preferred_element_type=jnp.float32,
    )
    shared_act = (
        jax.nn.silu(shared_mid[:, :shared_hidden]) * shared_mid[:, shared_hidden:]
    ).astype(jnp.bfloat16)
    shared_y = jnp.dot(
        shared_act,
        shared_out,
        preferred_element_type=jnp.float32,
    )
    shared_y = lax.optimization_barrier(shared_y)
    return (hidden_f + shared_y + routed).astype(jnp.bfloat16)


def solution(mesh):
    placed = (
        P(("group", "expert"), None),
        P(("group", "expert"), None),
        P("group", None),
        P(),
        P(),
        P("group", None),
        P(None, "group"),
        P("expert", None, None),
        P("expert", None, None),
        P(("group", "expert"), None),
    )
    return jax.shard_map(
        per_device,
        mesh=mesh,
        in_specs=placed,
        out_specs=P(("group", "expert"), None),
        check_vma=False,
    )
```

```python
import jax
import jax.numpy as jnp
from jax import lax
from jax.sharding import PartitionSpec as P
from jax.experimental import pallas as pl


def swiglu_rows(rows, w_in, w_out):
    width = w_out.shape[0]
    mid = jnp.dot(rows, w_in, preferred_element_type=jnp.float32)
    act = (jax.nn.silu(mid[:, :width]) * mid[:, width:]).astype(jnp.bfloat16)
    return jnp.dot(act, w_out, preferred_element_type=jnp.float32)


def gather_rows_by_chip(w, passenger):
    groups = lax.axis_size("group")
    ring = groups // 2
    g = lax.axis_index("group")
    y, c = g // 2, g % 2

    def shift(x, s):
        pairs = [(2 * q + k, 2 * ((q + s) % ring) + k) for q in range(ring) for k in range(2)]
        return lax.ppermute(x, "group", pairs)

    def sib(x):
        return lax.ppermute(x, "group", [(i, i ^ 1) for i in range(groups)])

    half = w.shape[0] // 2
    from_left = shift(w, 1)
    from_right = shift(w, -1)
    from_left, passenger = lax.optimization_barrier((from_left, passenger))
    far = jnp.concatenate(
        [shift(from_right[:half], -1), shift(from_left[half:], 1)], axis=0
    )
    pieces = [w, from_left, from_right, far, sib(w), sib(from_left), sib(from_right), sib(far)]
    return pieces, passenger


def chip_gather_order():
    ring = lax.axis_size("group") // 2
    g = lax.axis_index("group")
    y, c = g // 2, g % 2
    ys = (y + jnp.array([0, -1, 1, 2], jnp.int32) + ring) % ring
    return jnp.concatenate([2 * ys + c, 2 * ys + 1 - c])


def _attn_norm_kernel(ctx_ref, res_ref, gain_ref, *refs):
    hid_ref, normed_ref = refs[-2:]
    pieces = refs[:-2]
    width = pieces[0].shape[0]
    acc = None
    for i, piece in enumerate(pieces):
        term = jnp.dot(
            ctx_ref[:, i * width:(i + 1) * width], piece[...], preferred_element_type=jnp.float32
        )
        acc = term if acc is None else acc + term
    hidden = (res_ref[...].astype(jnp.float32) + acc).astype(jnp.bfloat16).astype(jnp.float32)
    scale = lax.rsqrt(jnp.mean(hidden * hidden, axis=-1, keepdims=True) + 1e-06)
    hid_ref[...] = hidden
    normed_ref[...] = (hidden * scale * gain_ref[...]).astype(jnp.bfloat16)


def attn_norm(ctx, pieces, residual, norm_gain):
    shape = (ctx.shape[0], pieces[0].shape[1])
    return pl.pallas_call(
        _attn_norm_kernel,
        out_shape=(
            jax.ShapeDtypeStruct(shape, jnp.float32),
            jax.ShapeDtypeStruct(shape, jnp.bfloat16),
        ),
    )(ctx, residual, norm_gain.reshape(1, -1), *pieces)


def per_device(
    context,
    residual,
    attn_out_w,
    norm_gain,
    router_w,
    shared_in,
    shared_out,
    expert_in,
    expert_out_w,
    routes,
):
    tok_rows = residual.shape[0]
    width = residual.shape[1]
    picks = routes.shape[1]
    experts = lax.axis_size("expert")
    capacity = 4 * tok_rows * picks // (3 * experts)
    slots = experts * capacity
    flat_e = routes.reshape(-1)
    onehot = (flat_e[:, None] == jnp.arange(experts, dtype=jnp.int32)[None, :]).astype(jnp.int32)
    rank = jnp.cumsum(onehot, axis=0) - onehot
    position = jnp.sum(rank * onehot, axis=1)
    slot_of = (flat_e * capacity + position).reshape(tok_rows, picks)
    hit = slot_of[:, :, None] == jnp.arange(slots, dtype=jnp.int32)[None, None, :]
    dispatch = jnp.any(hit, axis=1).astype(jnp.bfloat16)
    block = attn_out_w.shape[0]
    groups = lax.axis_size("group")
    if groups == 8:
        src = chip_gather_order()[:, None] * block + jnp.arange(block, dtype=jnp.int32)[None, :]
        perm = (jnp.arange(context.shape[1], dtype=jnp.int32)[:, None] == src.reshape(1, -1))
        ctx_perm = jnp.dot(context, perm.astype(jnp.bfloat16), preferred_element_type=jnp.float32)
        ctx_perm = ctx_perm.astype(jnp.bfloat16)
        pieces, (slot_of, dispatch, ctx_perm) = gather_rows_by_chip(
            attn_out_w, (slot_of, dispatch, ctx_perm)
        )
    else:
        pieces = [lax.all_gather(attn_out_w, "group", axis=0, tiled=True)]
        ctx_perm = context
    pieces, shared_in = lax.optimization_barrier((pieces, shared_in))
    shared_in = lax.all_gather(shared_in, "group", axis=0, tiled=True)
    hidden_f, normed = attn_norm(ctx_perm, pieces, residual, norm_gain)
    logits = jnp.dot(normed, router_w, preferred_element_type=jnp.float32)
    chosen = routes[:, :, None] == jnp.arange(experts, dtype=jnp.int32)[None, None, :]
    picked = jnp.sum(jnp.where(chosen, logits[:, None, :], 0.0), axis=-1)
    sig = jax.nn.sigmoid(picked)
    gates = sig / jnp.sum(sig, axis=1, keepdims=True)
    outgoing = jnp.dot(dispatch.T, normed, preferred_element_type=jnp.float32)
    outgoing = outgoing.astype(jnp.bfloat16).reshape(experts, capacity, width)
    hit = slot_of[:, :, None] == jnp.arange(slots, dtype=jnp.int32)[None, None, :]
    combine = jnp.sum(jnp.where(hit, gates[:, :, None], 0.0), axis=1)
    combine_hi = combine.astype(jnp.bfloat16)
    combine_lo = (combine - combine_hi.astype(jnp.float32)).astype(jnp.bfloat16)
    local_in = expert_in[0]
    local_out = expert_out_w[0]
    arrived = lax.all_to_all(outgoing, "expert", split_axis=0, concat_axis=0, tiled=True)
    arrived, shared_out = lax.optimization_barrier((arrived, shared_out))
    shared_out = lax.all_gather(shared_out, "group", axis=1, tiled=True)
    flat_rows = arrived.reshape(-1, width)
    expert_rows = swiglu_rows(flat_rows, local_in, local_out).astype(jnp.bfloat16)
    expert_rows, shared_in = lax.optimization_barrier((expert_rows, shared_in))
    returned = lax.all_to_all(
        expert_rows.reshape(arrived.shape),
        "expert",
        split_axis=0,
        concat_axis=0,
        tiled=True,
    )
    returned = returned.reshape(slots, width)
    both = jnp.dot(
        jnp.concatenate([combine_hi, combine_lo], axis=0), returned, preferred_element_type=jnp.float32
    )
    routed = both[:tok_rows] + both[tok_rows:]
    shared_hidden = shared_out.shape[0]
    shared_mid = jnp.dot(
        normed,
        shared_in,
        preferred_element_type=jnp.float32,
    )
    shared_act = (
        jax.nn.silu(shared_mid[:, :shared_hidden]) * shared_mid[:, shared_hidden:]
    ).astype(jnp.bfloat16)
    shared_y = jnp.dot(
        shared_act,
        shared_out,
        preferred_element_type=jnp.float32,
    )
    shared_y = lax.optimization_barrier(shared_y)
    return (hidden_f + shared_y + routed).astype(jnp.bfloat16)


def solution(mesh):
    placed = (
        P(("group", "expert"), None),
        P(("group", "expert"), None),
        P("group", None),
        P(),
        P(),
        P("group", None),
        P(None, "group"),
        P("expert", None, None),
        P("expert", None, None),
        P(("group", "expert"), None),
    )
    return jax.shard_map(
        per_device,
        mesh=mesh,
        in_specs=placed,
        out_specs=P(("group", "expert"), None),
        check_vma=False,
    )
```

```python
import jax
import jax.numpy as jnp
from jax import lax
from jax.sharding import PartitionSpec as P
from jax.experimental import pallas as pl


def swiglu_rows(rows, w_in, w_out):
    width = w_out.shape[0]
    mid = jnp.dot(rows, w_in, preferred_element_type=jnp.float32)
    act = (jax.nn.silu(mid[:, :width]) * mid[:, width:]).astype(jnp.bfloat16)
    return jnp.dot(act, w_out, preferred_element_type=jnp.float32)


def gather_rows_by_chip(w, passenger):
    groups = lax.axis_size("group")
    ring = groups // 2
    g = lax.axis_index("group")
    y, c = g // 2, g % 2

    def shift(x, s):
        pairs = [(2 * q + k, 2 * ((q + s) % ring) + k) for q in range(ring) for k in range(2)]
        return lax.ppermute(x, "group", pairs)

    def sib(x):
        return lax.ppermute(x, "group", [(i, i ^ 1) for i in range(groups)])

    half = w.shape[0] // 2
    from_left = shift(w, 1)
    from_right = shift(w, -1)
    from_left, passenger = lax.optimization_barrier((from_left, passenger))
    far = jnp.concatenate(
        [shift(from_right[:half], -1), shift(from_left[half:], 1)], axis=0
    )
    pieces = [w, from_left, from_right, far, sib(w), sib(from_left), sib(from_right), sib(far)]
    return pieces, passenger


def chip_gather_order():
    ring = lax.axis_size("group") // 2
    g = lax.axis_index("group")
    y, c = g // 2, g % 2
    ys = (y + jnp.array([0, -1, 1, 2], jnp.int32) + ring) % ring
    return jnp.concatenate([2 * ys + c, 2 * ys + 1 - c])


def _attn_norm_kernel(ctx_ref, res_ref, gain_ref, send_ref, *refs):
    hid_ref, normed_ref, out_ref = refs[-3:]
    pieces = refs[:-3]
    width = pieces[0].shape[0]
    acc = None
    for i, piece in enumerate(pieces):
        term = jnp.dot(
            ctx_ref[:, i * width:(i + 1) * width], piece[...], preferred_element_type=jnp.float32
        )
        acc = term if acc is None else acc + term
    hidden = (res_ref[...].astype(jnp.float32) + acc).astype(jnp.bfloat16).astype(jnp.float32)
    scale = lax.rsqrt(jnp.mean(hidden * hidden, axis=-1, keepdims=True) + 1e-06)
    hid_ref[...] = hidden
    normed = (hidden * scale * gain_ref[...]).astype(jnp.bfloat16)
    normed_ref[...] = normed
    out_ref[...] = jnp.dot(send_ref[...], normed, preferred_element_type=jnp.float32).astype(
        out_ref.dtype
    )


def attn_norm(ctx, pieces, residual, norm_gain, send):
    shape = (ctx.shape[0], pieces[0].shape[1])
    return pl.pallas_call(
        _attn_norm_kernel,
        out_shape=(
            jax.ShapeDtypeStruct(shape, jnp.float32),
            jax.ShapeDtypeStruct(shape, jnp.bfloat16),
            jax.ShapeDtypeStruct((send.shape[0], shape[1]), jnp.bfloat16),
        ),
    )(ctx, residual, norm_gain.reshape(1, -1), send, *pieces)


def per_device(
    context,
    residual,
    attn_out_w,
    norm_gain,
    router_w,
    shared_in,
    shared_out,
    expert_in,
    expert_out_w,
    routes,
):
    tok_rows = residual.shape[0]
    width = residual.shape[1]
    picks = routes.shape[1]
    experts = lax.axis_size("expert")
    capacity = 4 * tok_rows * picks // (3 * experts)
    slots = experts * capacity
    flat_e = routes.reshape(-1)
    onehot = (flat_e[:, None] == jnp.arange(experts, dtype=jnp.int32)[None, :]).astype(jnp.int32)
    rank = jnp.cumsum(onehot, axis=0) - onehot
    position = jnp.sum(rank * onehot, axis=1)
    slot_of = (flat_e * capacity + position).reshape(tok_rows, picks)
    dispatch = jnp.any(slot_of[None, :, :] == jnp.arange(slots, dtype=jnp.int32)[:, None, None], axis=2)
    dispatch = dispatch.astype(jnp.bfloat16)
    block = attn_out_w.shape[0]
    groups = lax.axis_size("group")
    if groups == 8:
        src = chip_gather_order()[:, None] * block + jnp.arange(block, dtype=jnp.int32)[None, :]
        perm = (jnp.arange(context.shape[1], dtype=jnp.int32)[:, None] == src.reshape(1, -1))
        ctx_perm = jnp.dot(context, perm.astype(jnp.bfloat16), preferred_element_type=jnp.float32)
        ctx_perm = ctx_perm.astype(jnp.bfloat16)
        pieces, (slot_of, dispatch, ctx_perm) = gather_rows_by_chip(
            attn_out_w, (slot_of, dispatch, ctx_perm)
        )
    else:
        pieces = [lax.all_gather(attn_out_w, "group", axis=0, tiled=True)]
        ctx_perm = context
    pieces, shared_in, shared_out = lax.optimization_barrier((pieces, shared_in, shared_out))
    shared_in = lax.all_gather(shared_in, "group", axis=0, tiled=True)
    shared_out = lax.all_gather(shared_out, "group", axis=1, tiled=True)
    hidden_f, normed, outgoing = attn_norm(ctx_perm, pieces, residual, norm_gain, dispatch)
    logits = jnp.dot(normed, router_w, preferred_element_type=jnp.float32)
    chosen = routes[:, :, None] == jnp.arange(experts, dtype=jnp.int32)[None, None, :]
    picked = jnp.sum(jnp.where(chosen, logits[:, None, :], 0.0), axis=-1)
    sig = jax.nn.sigmoid(picked)
    gates = sig / jnp.sum(sig, axis=1, keepdims=True)
    outgoing = outgoing.reshape(experts, capacity, width)
    hit = slot_of[:, :, None] == jnp.arange(slots, dtype=jnp.int32)[None, None, :]
    combine = jnp.sum(jnp.where(hit, gates[:, :, None], 0.0), axis=1)
    combine_hi = combine.astype(jnp.bfloat16)
    combine_lo = (combine - combine_hi.astype(jnp.float32)).astype(jnp.bfloat16)
    local_in = expert_in[0]
    local_out = expert_out_w[0]
    arrived = lax.all_to_all(outgoing, "expert", split_axis=0, concat_axis=0, tiled=True)
    flat_rows = arrived.reshape(-1, width)
    expert_rows = swiglu_rows(flat_rows, local_in, local_out).astype(jnp.bfloat16)
    expert_rows, shared_in, shared_out = lax.optimization_barrier((expert_rows, shared_in, shared_out))
    returned = lax.all_to_all(
        expert_rows.reshape(arrived.shape),
        "expert",
        split_axis=0,
        concat_axis=0,
        tiled=True,
    )
    returned = returned.reshape(slots, width)
    both = jnp.dot(
        jnp.concatenate([combine_hi, combine_lo], axis=0), returned, preferred_element_type=jnp.float32
    )
    routed = both[:tok_rows] + both[tok_rows:]
    shared_hidden = shared_out.shape[0]
    shared_mid = jnp.dot(
        normed,
        shared_in,
        preferred_element_type=jnp.float32,
    )
    shared_act = (
        jax.nn.silu(shared_mid[:, :shared_hidden]) * shared_mid[:, shared_hidden:]
    ).astype(jnp.bfloat16)
    shared_y = jnp.dot(
        shared_act,
        shared_out,
        preferred_element_type=jnp.float32,
    )
    shared_y = lax.optimization_barrier(shared_y)
    return (hidden_f + shared_y + routed).astype(jnp.bfloat16)


def solution(mesh):
    placed = (
        P(("group", "expert"), None),
        P(("group", "expert"), None),
        P("group", None),
        P(),
        P(),
        P("group", None),
        P(None, "group"),
        P("expert", None, None),
        P("expert", None, None),
        P(("group", "expert"), None),
    )
    return jax.shard_map(
        per_device,
        mesh=mesh,
        in_specs=placed,
        out_specs=P(("group", "expert"), None),
        check_vma=False,
    )
```

```python
import jax
import jax.numpy as jnp
from jax import lax
from jax.sharding import PartitionSpec as P
from jax.experimental import pallas as pl


def swiglu_rows(rows, w_in, w_out):
    width = w_out.shape[0]
    mid = jnp.dot(rows, w_in, preferred_element_type=jnp.float32)
    act = (jax.nn.silu(mid[:, :width]) * mid[:, width:]).astype(jnp.bfloat16)
    return jnp.dot(act, w_out, preferred_element_type=jnp.float32)


def gather_rows_by_chip(w, passenger):
    groups = lax.axis_size("group")
    ring = groups // 2
    g = lax.axis_index("group")
    y, c = g // 2, g % 2

    def shift(x, s):
        pairs = [(2 * q + k, 2 * ((q + s) % ring) + k) for q in range(ring) for k in range(2)]
        return lax.ppermute(x, "group", pairs)

    def sib(x):
        return lax.ppermute(x, "group", [(i, i ^ 1) for i in range(groups)])

    from_left = shift(w, 1)
    from_right = shift(w, -1)
    from_left, passenger = lax.optimization_barrier((from_left, passenger))
    onward = jnp.where(c == 0, from_left, from_right)
    pairs = [(2 * q, 2 * ((q + 1) % ring)) for q in range(ring)]
    pairs += [(2 * q + 1, 2 * ((q - 1) % ring) + 1) for q in range(ring)]
    far = lax.ppermute(onward, "group", pairs)
    pieces = [w, from_left, from_right, far, sib(w), sib(from_left), sib(from_right), sib(far)]
    return pieces, passenger


def chip_gather_order():
    ring = lax.axis_size("group") // 2
    g = lax.axis_index("group")
    y, c = g // 2, g % 2
    ys = (y + jnp.array([0, -1, 1, 2], jnp.int32) + ring) % ring
    return jnp.concatenate([2 * ys + c, 2 * ys + 1 - c])


def _attn_norm_kernel(ctx_ref, res_ref, gain_ref, *refs):
    hid_ref, normed_ref = refs[-2:]
    pieces = refs[:-2]
    width = pieces[0].shape[0]
    acc = None
    for i, piece in enumerate(pieces):
        term = jnp.dot(
            ctx_ref[:, i * width:(i + 1) * width], piece[...], preferred_element_type=jnp.float32
        )
        acc = term if acc is None else acc + term
    hidden = (res_ref[...].astype(jnp.float32) + acc).astype(jnp.bfloat16).astype(jnp.float32)
    scale = lax.rsqrt(jnp.mean(hidden * hidden, axis=-1, keepdims=True) + 1e-06)
    hid_ref[...] = hidden
    normed_ref[...] = (hidden * scale * gain_ref[...]).astype(jnp.bfloat16)


def attn_norm(ctx, pieces, residual, norm_gain):
    shape = (ctx.shape[0], pieces[0].shape[1])
    return pl.pallas_call(
        _attn_norm_kernel,
        out_shape=(
            jax.ShapeDtypeStruct(shape, jnp.float32),
            jax.ShapeDtypeStruct(shape, jnp.bfloat16),
        ),
    )(ctx, residual, norm_gain.reshape(1, -1), *pieces)


def per_device(
    context,
    residual,
    attn_out_w,
    norm_gain,
    router_w,
    shared_in,
    shared_out,
    expert_in,
    expert_out_w,
    routes,
):
    tok_rows = residual.shape[0]
    width = residual.shape[1]
    picks = routes.shape[1]
    experts = lax.axis_size("expert")
    capacity = 4 * tok_rows * picks // (3 * experts)
    slots = experts * capacity
    flat_e = routes.reshape(-1)
    onehot = (flat_e[:, None] == jnp.arange(experts, dtype=jnp.int32)[None, :]).astype(jnp.int32)
    rank = jnp.cumsum(onehot, axis=0) - onehot
    position = jnp.sum(rank * onehot, axis=1)
    slot_of = (flat_e * capacity + position).reshape(tok_rows, picks)
    hit = slot_of[:, :, None] == jnp.arange(slots, dtype=jnp.int32)[None, None, :]
    dispatch = jnp.any(hit, axis=1).astype(jnp.bfloat16)
    block = attn_out_w.shape[0]
    groups = lax.axis_size("group")
    if groups == 8:
        src = chip_gather_order()[:, None] * block + jnp.arange(block, dtype=jnp.int32)[None, :]
        perm = (jnp.arange(context.shape[1], dtype=jnp.int32)[:, None] == src.reshape(1, -1))
        ctx_perm = jnp.dot(context, perm.astype(jnp.bfloat16), preferred_element_type=jnp.float32)
        ctx_perm = ctx_perm.astype(jnp.bfloat16)
        pieces, (slot_of, dispatch, ctx_perm) = gather_rows_by_chip(
            attn_out_w, (slot_of, dispatch, ctx_perm)
        )
    else:
        pieces = [lax.all_gather(attn_out_w, "group", axis=0, tiled=True)]
        ctx_perm = context
    pieces, shared_in, shared_out = lax.optimization_barrier((pieces, shared_in, shared_out))
    shared_in = lax.all_gather(shared_in, "group", axis=0, tiled=True)
    shared_out = lax.all_gather(shared_out, "group", axis=1, tiled=True)
    hidden_f, normed = attn_norm(ctx_perm, pieces, residual, norm_gain)
    logits = jnp.dot(normed, router_w, preferred_element_type=jnp.float32)
    chosen = routes[:, :, None] == jnp.arange(experts, dtype=jnp.int32)[None, None, :]
    picked = jnp.sum(jnp.where(chosen, logits[:, None, :], 0.0), axis=-1)
    sig = jax.nn.sigmoid(picked)
    gates = sig / jnp.sum(sig, axis=1, keepdims=True)
    outgoing = jnp.dot(dispatch.T, normed, preferred_element_type=jnp.float32)
    outgoing = outgoing.astype(jnp.bfloat16).reshape(experts, capacity, width)
    hit = slot_of[:, :, None] == jnp.arange(slots, dtype=jnp.int32)[None, None, :]
    combine = jnp.sum(jnp.where(hit, gates[:, :, None], 0.0), axis=1)
    combine_hi = combine.astype(jnp.bfloat16)
    combine_lo = (combine - combine_hi.astype(jnp.float32)).astype(jnp.bfloat16)
    local_in = expert_in[0]
    local_out = expert_out_w[0]
    arrived = lax.all_to_all(outgoing, "expert", split_axis=0, concat_axis=0, tiled=True)
    flat_rows = arrived.reshape(-1, width)
    expert_rows = swiglu_rows(flat_rows, local_in, local_out).astype(jnp.bfloat16)
    expert_rows, shared_in, shared_out = lax.optimization_barrier((expert_rows, shared_in, shared_out))
    returned = lax.all_to_all(
        expert_rows.reshape(arrived.shape),
        "expert",
        split_axis=0,
        concat_axis=0,
        tiled=True,
    )
    returned = returned.reshape(slots, width)
    both = jnp.dot(
        jnp.concatenate([combine_hi, combine_lo], axis=0), returned, preferred_element_type=jnp.float32
    )
    routed = both[:tok_rows] + both[tok_rows:]
    shared_hidden = shared_out.shape[0]
    shared_mid = jnp.dot(
        normed,
        shared_in,
        preferred_element_type=jnp.float32,
    )
    shared_act = (
        jax.nn.silu(shared_mid[:, :shared_hidden]) * shared_mid[:, shared_hidden:]
    ).astype(jnp.bfloat16)
    shared_y = jnp.dot(
        shared_act,
        shared_out,
        preferred_element_type=jnp.float32,
    )
    shared_y = lax.optimization_barrier(shared_y)
    return (hidden_f + shared_y + routed).astype(jnp.bfloat16)


def solution(mesh):
    placed = (
        P(("group", "expert"), None),
        P(("group", "expert"), None),
        P("group", None),
        P(),
        P(),
        P("group", None),
        P(None, "group"),
        P("expert", None, None),
        P("expert", None, None),
        P(("group", "expert"), None),
    )
    return jax.shard_map(
        per_device,
        mesh=mesh,
        in_specs=placed,
        out_specs=P(("group", "expert"), None),
        check_vma=False,
    )
```

```python
import jax
import jax.numpy as jnp
from jax import lax
from jax.sharding import PartitionSpec as P
from jax.experimental import pallas as pl


def swiglu_rows(rows, w_in, w_out):
    width = w_out.shape[0]
    mid = jnp.dot(rows, w_in, preferred_element_type=jnp.float32)
    act = (jax.nn.silu(mid[:, :width]) * mid[:, width:]).astype(jnp.bfloat16)
    return jnp.dot(act, w_out, preferred_element_type=jnp.float32)


def gather_rows_by_chip(w, passenger):
    groups = lax.axis_size("group")
    ring = groups // 2
    g = lax.axis_index("group")
    y, c = g // 2, g % 2

    def shift(x, s):
        pairs = [(2 * q + k, 2 * ((q + s) % ring) + k) for q in range(ring) for k in range(2)]
        return lax.ppermute(x, "group", pairs)

    def sib(x):
        return lax.ppermute(x, "group", [(i, i ^ 1) for i in range(groups)])

    def mirrored(x, s):
        pairs = [(2 * q, 2 * ((q + s) % ring)) for q in range(ring)]
        pairs += [(2 * q + 1, 2 * ((q - s) % ring) + 1) for q in range(ring)]
        return lax.ppermute(x, "group", pairs)

    near = mirrored(w, 1)
    other = mirrored(w, -1)
    near, passenger = lax.optimization_barrier((near, passenger))
    far = mirrored(near, 1)
    pieces = [w, near, other, far, sib(w), sib(near), sib(other), sib(far)]
    return pieces, passenger


def chip_gather_order():
    ring = lax.axis_size("group") // 2
    g = lax.axis_index("group")
    y, c = g // 2, g % 2
    s = 1 - 2 * c
    mine = (y + jnp.array([0, -1, 1, 2], jnp.int32) * jnp.array([1, s, s, 1], jnp.int32) + ring) % ring
    theirs = (y + jnp.array([0, 1, -1, 2], jnp.int32) * jnp.array([1, s, s, 1], jnp.int32) + ring) % ring
    return jnp.concatenate([2 * mine + c, 2 * theirs + 1 - c])


def _attn_norm_kernel(ctx_ref, res_ref, gain_ref, *refs):
    hid_ref, normed_ref = refs[-2:]
    pieces = refs[:-2]
    width = pieces[0].shape[0]
    acc = None
    for i, piece in enumerate(pieces):
        term = jnp.dot(
            ctx_ref[:, i * width:(i + 1) * width], piece[...], preferred_element_type=jnp.float32
        )
        acc = term if acc is None else acc + term
    hidden = (res_ref[...].astype(jnp.float32) + acc).astype(jnp.bfloat16).astype(jnp.float32)
    scale = lax.rsqrt(jnp.mean(hidden * hidden, axis=-1, keepdims=True) + 1e-06)
    hid_ref[...] = hidden
    normed_ref[...] = (hidden * scale * gain_ref[...]).astype(jnp.bfloat16)


def attn_norm(ctx, pieces, residual, norm_gain):
    shape = (ctx.shape[0], pieces[0].shape[1])
    return pl.pallas_call(
        _attn_norm_kernel,
        out_shape=(
            jax.ShapeDtypeStruct(shape, jnp.float32),
            jax.ShapeDtypeStruct(shape, jnp.bfloat16),
        ),
    )(ctx, residual, norm_gain.reshape(1, -1), *pieces)


def per_device(
    context,
    residual,
    attn_out_w,
    norm_gain,
    router_w,
    shared_in,
    shared_out,
    expert_in,
    expert_out_w,
    routes,
):
    tok_rows = residual.shape[0]
    width = residual.shape[1]
    picks = routes.shape[1]
    experts = lax.axis_size("expert")
    capacity = 4 * tok_rows * picks // (3 * experts)
    slots = experts * capacity
    flat_e = routes.reshape(-1)
    onehot = (flat_e[:, None] == jnp.arange(experts, dtype=jnp.int32)[None, :]).astype(jnp.int32)
    rank = jnp.cumsum(onehot, axis=0) - onehot
    position = jnp.sum(rank * onehot, axis=1)
    slot_of = (flat_e * capacity + position).reshape(tok_rows, picks)
    hit = slot_of[:, :, None] == jnp.arange(slots, dtype=jnp.int32)[None, None, :]
    dispatch = jnp.any(hit, axis=1).astype(jnp.bfloat16)
    block = attn_out_w.shape[0]
    groups = lax.axis_size("group")
    if groups == 8:
        src = chip_gather_order()[:, None] * block + jnp.arange(block, dtype=jnp.int32)[None, :]
        perm = (jnp.arange(context.shape[1], dtype=jnp.int32)[:, None] == src.reshape(1, -1))
        ctx_perm = jnp.dot(context, perm.astype(jnp.bfloat16), preferred_element_type=jnp.float32)
        ctx_perm = ctx_perm.astype(jnp.bfloat16)
        pieces, (slot_of, dispatch, ctx_perm) = gather_rows_by_chip(
            attn_out_w, (slot_of, dispatch, ctx_perm)
        )
    else:
        pieces = [lax.all_gather(attn_out_w, "group", axis=0, tiled=True)]
        ctx_perm = context
    pieces, shared_in, shared_out = lax.optimization_barrier((pieces, shared_in, shared_out))
    shared_in = lax.all_gather(shared_in, "group", axis=0, tiled=True)
    shared_out = lax.all_gather(shared_out, "group", axis=1, tiled=True)
    hidden_f, normed = attn_norm(ctx_perm, pieces, residual, norm_gain)
    logits = jnp.dot(normed, router_w, preferred_element_type=jnp.float32)
    chosen = routes[:, :, None] == jnp.arange(experts, dtype=jnp.int32)[None, None, :]
    picked = jnp.sum(jnp.where(chosen, logits[:, None, :], 0.0), axis=-1)
    sig = jax.nn.sigmoid(picked)
    gates = sig / jnp.sum(sig, axis=1, keepdims=True)
    outgoing = jnp.dot(dispatch.T, normed, preferred_element_type=jnp.float32)
    outgoing = outgoing.astype(jnp.bfloat16).reshape(experts, capacity, width)
    hit = slot_of[:, :, None] == jnp.arange(slots, dtype=jnp.int32)[None, None, :]
    combine = jnp.sum(jnp.where(hit, gates[:, :, None], 0.0), axis=1)
    combine_hi = combine.astype(jnp.bfloat16)
    combine_lo = (combine - combine_hi.astype(jnp.float32)).astype(jnp.bfloat16)
    local_in = expert_in[0]
    local_out = expert_out_w[0]
    arrived = lax.all_to_all(outgoing, "expert", split_axis=0, concat_axis=0, tiled=True)
    flat_rows = arrived.reshape(-1, width)
    expert_rows = swiglu_rows(flat_rows, local_in, local_out).astype(jnp.bfloat16)
    expert_rows, shared_in, shared_out = lax.optimization_barrier((expert_rows, shared_in, shared_out))
    returned = lax.all_to_all(
        expert_rows.reshape(arrived.shape),
        "expert",
        split_axis=0,
        concat_axis=0,
        tiled=True,
    )
    returned = returned.reshape(slots, width)
    both = jnp.dot(
        jnp.concatenate([combine_hi, combine_lo], axis=0), returned, preferred_element_type=jnp.float32
    )
    routed = both[:tok_rows] + both[tok_rows:]
    shared_hidden = shared_out.shape[0]
    shared_mid = jnp.dot(
        normed,
        shared_in,
        preferred_element_type=jnp.float32,
    )
    shared_act = (
        jax.nn.silu(shared_mid[:, :shared_hidden]) * shared_mid[:, shared_hidden:]
    ).astype(jnp.bfloat16)
    shared_y = jnp.dot(
        shared_act,
        shared_out,
        preferred_element_type=jnp.float32,
    )
    shared_y = lax.optimization_barrier(shared_y)
    return (hidden_f + shared_y + routed).astype(jnp.bfloat16)


def solution(mesh):
    placed = (
        P(("group", "expert"), None),
        P(("group", "expert"), None),
        P("group", None),
        P(),
        P(),
        P("group", None),
        P(None, "group"),
        P("expert", None, None),
        P("expert", None, None),
        P(("group", "expert"), None),
    )
    return jax.shard_map(
        per_device,
        mesh=mesh,
        in_specs=placed,
        out_specs=P(("group", "expert"), None),
        check_vma=False,
    )
```

```python
import jax
import jax.numpy as jnp
from jax import lax
from jax.sharding import PartitionSpec as P
from jax.experimental import pallas as pl


def swiglu_rows(rows, w_in, w_out):
    width = w_out.shape[0]
    mid = jnp.dot(rows, w_in, preferred_element_type=jnp.float32)
    act = (jax.nn.silu(mid[:, :width]) * mid[:, width:]).astype(jnp.bfloat16)
    return jnp.dot(act, w_out, preferred_element_type=jnp.float32)


def gather_rows_by_chip(w, passenger):
    groups = lax.axis_size("group")
    ring = groups // 2
    g = lax.axis_index("group")
    y, c = g // 2, g % 2

    def shift(x, s):
        pairs = [(2 * q + k, 2 * ((q + s) % ring) + k) for q in range(ring) for k in range(2)]
        return lax.ppermute(x, "group", pairs)

    def sib(x):
        return lax.ppermute(x, "group", [(i, i ^ 1) for i in range(groups)])

    def mirrored(x, s):
        pairs = [(2 * q, 2 * ((q + s) % ring)) for q in range(ring)]
        pairs += [(2 * q + 1, 2 * ((q - s) % ring) + 1) for q in range(ring)]
        return lax.ppermute(x, "group", pairs)

    near = mirrored(w, 1)
    other = mirrored(w, -1)
    near, passenger = lax.optimization_barrier((near, passenger))
    far = mirrored(near, 1)
    pieces = [w, near, other, far, sib(w), sib(near), sib(other), sib(far)]
    return pieces, passenger


def chip_gather_order():
    ring = lax.axis_size("group") // 2
    g = lax.axis_index("group")
    y, c = g // 2, g % 2
    s = 1 - 2 * c
    mine = (y + jnp.array([0, -1, 1, 2], jnp.int32) * jnp.array([1, s, s, 1], jnp.int32) + ring) % ring
    theirs = (y + jnp.array([0, 1, -1, 2], jnp.int32) * jnp.array([1, s, s, 1], jnp.int32) + ring) % ring
    return jnp.concatenate([2 * mine + c, 2 * theirs + 1 - c])


def _attn_norm_kernel(ctx_ref, res_ref, gain_ref, *refs):
    hid_ref, normed_ref = refs[-2:]
    pieces = refs[:-2]
    width = pieces[0].shape[0]
    acc = None
    for i, piece in enumerate(pieces):
        term = jnp.dot(
            ctx_ref[:, i * width:(i + 1) * width], piece[...], preferred_element_type=jnp.float32
        )
        acc = term if acc is None else acc + term
    hidden = (res_ref[...].astype(jnp.float32) + acc).astype(jnp.bfloat16).astype(jnp.float32)
    scale = lax.rsqrt(jnp.mean(hidden * hidden, axis=-1, keepdims=True) + 1e-06)
    hid_ref[...] = hidden
    normed_ref[...] = (hidden * scale * gain_ref[...]).astype(jnp.bfloat16)


def attn_norm(ctx, pieces, residual, norm_gain):
    shape = (ctx.shape[0], pieces[0].shape[1])
    return pl.pallas_call(
        _attn_norm_kernel,
        out_shape=(
            jax.ShapeDtypeStruct(shape, jnp.float32),
            jax.ShapeDtypeStruct(shape, jnp.bfloat16),
        ),
    )(ctx, residual, norm_gain.reshape(1, -1), *pieces)


def per_device(
    context,
    residual,
    attn_out_w,
    norm_gain,
    router_w,
    shared_in,
    shared_out,
    expert_in,
    expert_out_w,
    routes,
):
    tok_rows = residual.shape[0]
    width = residual.shape[1]
    picks = routes.shape[1]
    experts = lax.axis_size("expert")
    capacity = 4 * tok_rows * picks // (3 * experts)
    slots = experts * capacity
    flat_e = routes.reshape(-1)
    onehot = (flat_e[:, None] == jnp.arange(experts, dtype=jnp.int32)[None, :]).astype(jnp.int32)
    rank = jnp.cumsum(onehot, axis=0) - onehot
    position = jnp.sum(rank * onehot, axis=1)
    slot_of = (flat_e * capacity + position).reshape(tok_rows, picks)
    dispatch = jnp.any(slot_of[None, :, :] == jnp.arange(slots, dtype=jnp.int32)[:, None, None], axis=2)
    dispatch = dispatch.astype(jnp.bfloat16)
    block = attn_out_w.shape[0]
    groups = lax.axis_size("group")
    if groups == 8:
        src = chip_gather_order()[:, None] * block + jnp.arange(block, dtype=jnp.int32)[None, :]
        perm = (jnp.arange(context.shape[1], dtype=jnp.int32)[:, None] == src.reshape(1, -1))
        ctx_perm = jnp.dot(context, perm.astype(jnp.bfloat16), preferred_element_type=jnp.float32)
        ctx_perm = ctx_perm.astype(jnp.bfloat16)
        pieces, (slot_of, dispatch, ctx_perm) = gather_rows_by_chip(
            attn_out_w, (slot_of, dispatch, ctx_perm)
        )
    else:
        pieces = [lax.all_gather(attn_out_w, "group", axis=0, tiled=True)]
        ctx_perm = context
    pieces, shared_in, shared_out = lax.optimization_barrier((pieces, shared_in, shared_out))
    shared_in = lax.all_gather(shared_in, "group", axis=0, tiled=True)
    shared_out = lax.all_gather(shared_out, "group", axis=1, tiled=True)
    hidden_f, normed = attn_norm(ctx_perm, pieces, residual, norm_gain)
    logits = jnp.dot(normed, router_w, preferred_element_type=jnp.float32)
    chosen = routes[:, :, None] == jnp.arange(experts, dtype=jnp.int32)[None, None, :]
    picked = jnp.sum(jnp.where(chosen, logits[:, None, :], 0.0), axis=-1)
    sig = jax.nn.sigmoid(picked)
    gates = sig / jnp.sum(sig, axis=1, keepdims=True)
    outgoing = jnp.dot(dispatch, normed, preferred_element_type=jnp.float32)
    outgoing = outgoing.astype(jnp.bfloat16).reshape(experts, capacity, width)
    hit = slot_of[:, :, None] == jnp.arange(slots, dtype=jnp.int32)[None, None, :]
    combine = jnp.sum(jnp.where(hit, gates[:, :, None], 0.0), axis=1)
    combine_hi = combine.astype(jnp.bfloat16)
    combine_lo = (combine - combine_hi.astype(jnp.float32)).astype(jnp.bfloat16)
    local_in = expert_in[0]
    local_out = expert_out_w[0]
    arrived = lax.all_to_all(outgoing, "expert", split_axis=0, concat_axis=0, tiled=True)
    flat_rows = arrived.reshape(-1, width)
    expert_rows = swiglu_rows(flat_rows, local_in, local_out).astype(jnp.bfloat16)
    expert_rows, shared_in, shared_out = lax.optimization_barrier((expert_rows, shared_in, shared_out))
    returned = lax.all_to_all(
        expert_rows.reshape(arrived.shape),
        "expert",
        split_axis=0,
        concat_axis=0,
        tiled=True,
    )
    returned = returned.reshape(slots, width)
    both = jnp.dot(
        jnp.concatenate([combine_hi, combine_lo], axis=0), returned, preferred_element_type=jnp.float32
    )
    routed = both[:tok_rows] + both[tok_rows:]
    shared_hidden = shared_out.shape[0]
    shared_mid = jnp.dot(
        normed,
        shared_in,
        preferred_element_type=jnp.float32,
    )
    shared_act = (
        jax.nn.silu(shared_mid[:, :shared_hidden]) * shared_mid[:, shared_hidden:]
    ).astype(jnp.bfloat16)
    shared_y = jnp.dot(
        shared_act,
        shared_out,
        preferred_element_type=jnp.float32,
    )
    shared_y = lax.optimization_barrier(shared_y)
    return (hidden_f + shared_y + routed).astype(jnp.bfloat16)


def solution(mesh):
    placed = (
        P(("group", "expert"), None),
        P(("group", "expert"), None),
        P("group", None),
        P(),
        P(),
        P("group", None),
        P(None, "group"),
        P("expert", None, None),
        P("expert", None, None),
        P(("group", "expert"), None),
    )
    return jax.shard_map(
        per_device,
        mesh=mesh,
        in_specs=placed,
        out_specs=P(("group", "expert"), None),
        check_vma=False,
    )
```
